128 devices in a mesh: section: 2 (over x_lo), owner: 8 (over x_hi, z), pos: 8 (over y, core).
Axes of the slice: x: 4 (x_hi: 2, x_lo: 2; x = x_hi * 2 + x_lo), y: 4, z: 4, core: 2. Of those that a mesh axis runs over, the one named last changes fastest.
Arguments:
- hidden_rows: bfloat16 [2, 131072, 1024], P(None, ('owner', 'pos'), 'section'), may hold values from -144 to 144
- w_proj: bfloat16 [1024, 256], P('section'), may hold values from -0.1875 to 0.1875
- panels: bfloat16 [8192, 256], P(('section', 'owner')), may hold values from -1.5 to 1.5
- cand_ids: int32 [8192], P(('section', 'owner')), may hold values from 0 to 65535
- counts: int32 [65536], replicated, may hold values from 1 to 65535
- target_slot: int32 [262144], P(('section', 'owner', 'pos')), may hold values from 0 to 8191
- block_lists: int32 [1024, 12], P(('section', 'owner', 'pos')), may hold values from 0 to 31, all different within a row
- list_lens: int32 [1024], P(('section', 'owner', 'pos')), may hold values from 1 to 12, 7680 in all
Outputs:
- query_grad: bfloat16 [262144, 256], P(('section', 'owner', 'pos'))
- position_loss: float32 [262144], P(('section', 'owner', 'pos'))
- trunk_grad: bfloat16 [2, 131072, 1024], P(None, ('owner', 'pos'), 'section')
The draws below stay inside these ranges and needn't reach their ends.
Inputs may be any that keep to these rules, and one draw needn't show every extreme that they name: `block_lists`: each row names 12 different candidate blocks. `list_lens`: entries of a row of block_lists past its length are padding and not scored.
All inputs are finite; a program needn't handle non-finite values. No bound on the sum of `list_lens` on one device may be relied on, other than what follows from the above.
Results may differ from the reference program's by a relative error of at most 0.012.
The reference program's roundings to bfloat16 on the way count: a program that leaves them out, or rounds other values in their place, can miss the bound.
Values may be sent and summed in bfloat16 or wider, within the bound.
No kernel may reach another device: no remote copies, remote signals or barrier semaphores. Data moves between devices by JAX's collectives and lax.ppermute only.
A program may use at most 64 MiB of HBM per device.

```python
import math
import jax
import jax.numpy as jnp
import numpy as np
from jax import lax

D = 1024
E = 256
BLOCK = 256
LIST = 12
ITEMS = 65536
TOKENS = 262144
PBLOCKS = 1024
CANDS = 8192
NB = 32


def draw_hidden_rows(key, part):
    first_key = jax.random.fold_in(key, 0)
    values = jnp.clip(jax.random.normal(first_key, (2, TOKENS // 2, D), jnp.float32), -6.0, 6.0)
    return values.astype(jnp.bfloat16)


def set_ends(array, own_key, least, top_value):
    extent = array.shape
    index_at = [jax.random.randint(jax.random.fold_in(own_key, axis), (), 0, extent[axis]) for axis in range(len(extent))]
    array = array.at[tuple(index_at)].set(least)
    longest = extent.index(max(extent))
    index_at[longest] = (index_at[longest] + 1) % extent[longest]
    return array.at[tuple(index_at)].set(top_value)


def shard_levels(own_key, extent, pieces, low, high):
    loudness, own = 1.0, jax.random.fold_in(own_key, 6)
    for position, shards_of in pieces:
        steps = jnp.exp(jax.random.uniform(jax.random.fold_in(own, position), (shards_of,), jnp.float32, low / len(pieces), high / len(pieces)))
        loudness = loudness * jnp.repeat(steps, extent[position] // shards_of).reshape([-1 if axis == position else 1 for axis in range(len(extent))])
    return loudness


def distinct(stream_key, rows, amount, top, lift):
    order = jax.random.permutation(jax.random.fold_in(stream_key, 1), amount)
    favour = order
    for power in range(3):
        favour = favour * favour // amount
    favour = favour * lift // amount
    tickets = jax.random.randint(jax.random.fold_in(stream_key, 2), (rows, amount), 0, 4096) + favour
    holders = jax.random.permutation(jax.random.fold_in(stream_key, 3), rows)[jnp.arange(amount) % rows]
    tickets = jnp.where(jnp.arange(rows)[:, None] == holders[None, :], 1 << 14, tickets)
    score = tickets * amount + jnp.arange(amount)
    return lax.top_k(score.astype(jnp.int32), top)[1].astype(jnp.int32)


def length_profile(amount, total, reach, slope):
    portions = [(1 << 20) // math.isqrt(grade ** slope) + 1 for grade in range(2, amount + 1)]
    spare, given = total - reach - (amount - 1), [1] * (amount - 1)
    while spare > 0:
        movable = [i for i in range(amount - 1) if given[i] < reach]
        pool, left = sum([portions[i] for i in movable]), spare
        for i in movable:
            addition = min(reach - given[i], max(1, left * portions[i] // pool), spare)
            given[i] = given[i] + addition
            spare = spare - addition
    return np.array([reach] + given)


def uneven_parts(key, amount, total, bound, skew):
    if amount == 2:
        one = jax.random.randint(key, (), max(1, total - bound), min(bound, total - 1) + 1)
        return jnp.stack([one, total - one])
    tallies = jnp.asarray(length_profile(amount, total, bound, skew), jnp.int32)
    couples = (amount - 1) // 2
    giver, taker = tallies[1:1 + 2 * couples:2], tallies[2:2 + 2 * couples:2]
    room = jnp.minimum(giver - 1, bound - taker)
    passed = jax.random.randint(jax.random.fold_in(key, 1), (couples,), 0, 1 << 20) % (room + 1)
    tallies = tallies.at[1:1 + 2 * couples:2].set(giver - passed).at[2:2 + 2 * couples:2].set(taker + passed)
    return tallies[jax.random.permutation(jax.random.fold_in(key, 2), amount)]


def gaussian(key, extent, scale, limit, shards=(), held_as=jnp.bfloat16):
    result = scale * jax.random.normal(key, extent, jnp.float32)
    if shards:
        result = result * shard_levels(key, extent, shards, -0.22, 0.18)
    return jnp.clip(result, -limit, limit).astype(held_as)


def setup_inputs(seed: int = 0) -> dict:
    key_of = jax.random.split(jax.random.key(seed), 9)
    hidden_rows = draw_hidden_rows(jax.random.fold_in(key_of[8], 71), 0)
    w_proj = gaussian(key_of[1], (D, E), D ** -0.5, 0.1875, ((0, 2),))
    panels = gaussian(key_of[2], (CANDS, E), 0.25, 1.5, ((0, 16),))
    cand_ids = set_ends(jax.random.randint(key_of[3], (CANDS,), 0, ITEMS), jax.random.fold_in(key_of[3], 1), 0, ITEMS - 1).astype(jnp.int32)
    counts = set_ends(jax.random.randint(key_of[4], (ITEMS,), 1, 65536), jax.random.fold_in(key_of[4], 1), 1, 65535).astype(jnp.int32)
    target_slot = set_ends(jax.random.randint(key_of[5], (TOKENS,), 0, CANDS), jax.random.fold_in(key_of[5], 1), 0, CANDS - 1).astype(jnp.int32)
    block_lists = distinct(key_of[6], PBLOCKS, NB, LIST, 6144)
    list_lens = uneven_parts(key_of[7], PBLOCKS, PBLOCKS * LIST * 5 // 8, LIST, 2).astype(jnp.int32)
    return {"hidden_rows": hidden_rows, "w_proj": w_proj, "panels": panels, "cand_ids": cand_ids, "counts": counts, "target_slot": target_slot, "block_lists": block_lists, "list_lens": list_lens}


NEG_FILL = -1.0e30


def reference(hidden_rows, w_proj, panels, cand_ids, counts, target_slot, block_lists, list_lens):
    trunk_rows = hidden_rows.reshape(TOKENS, D)
    queries = jnp.dot(trunk_rows, w_proj, preferred_element_type=jnp.float32).astype(jnp.bfloat16)
    log_counts = jnp.log(counts[cand_ids].astype(jnp.float32)).astype(jnp.bfloat16)
    cand_blocks = panels.reshape(NB, BLOCK, E)
    bias_blocks = log_counts.reshape(NB, BLOCK)
    offsets = jnp.arange(BLOCK, dtype=jnp.int32)
    entries = jnp.arange(LIST, dtype=jnp.int32)

    def one_block(inputs):
        query_rows, targets, listed, length = inputs
        query_wide = query_rows.astype(jnp.float32)
        positive = panels[targets].astype(jnp.float32)
        pos_logit = jnp.sum(query_wide * positive, axis=1) - log_counts[targets].astype(jnp.float32)
        candidates = cand_blocks[listed].astype(jnp.float32)
        logits = jnp.einsum("re,kce->rkc", query_wide, candidates) - bias_blocks[listed].astype(jnp.float32)[None, :, :]
        slot_ids = listed[:, None] * BLOCK + offsets[None, :]
        usable = (slot_ids[None, :, :] != targets[:, None, None]) & (entries < length)[None, :, None]
        masked = jnp.where(usable, logits, NEG_FILL)
        row_max = jnp.maximum(pos_logit, jnp.max(masked, axis=(1, 2)))
        row_sum = jnp.exp(pos_logit - row_max) + jnp.sum(jnp.where(usable, jnp.exp(masked - row_max[:, None, None]), 0.0), axis=(1, 2))
        log_total = row_max + jnp.log(row_sum)
        weights = jnp.where(usable, jnp.exp(masked - log_total[:, None, None]), 0.0).astype(jnp.bfloat16)
        weighted = jnp.einsum("rkc,kce->re", weights.astype(jnp.float32), candidates)
        query_grad = weighted + (jnp.exp(pos_logit - log_total) - 1.0)[:, None] * positive
        return query_grad.astype(jnp.bfloat16), log_total - pos_logit

    query_grad, position_loss = lax.map(one_block, (queries.reshape(PBLOCKS, BLOCK, E), target_slot.reshape(PBLOCKS, BLOCK), block_lists, list_lens))
    query_grad = query_grad.reshape(TOKENS, E)
    trunk_grad = jnp.dot(query_grad, w_proj.T, preferred_element_type=jnp.float32).astype(jnp.bfloat16)
    return query_grad, position_loss.reshape(TOKENS), trunk_grad.reshape(2, TOKENS // 2, D)
```

```python
import functools

import jax
import jax.numpy as jnp
from jax import lax
from jax.experimental import pallas as pl
from jax.experimental.pallas import tpu as pltpu
from jax.sharding import PartitionSpec as P

BLOCK = 256
NEG_FILL = -1e30
BIAS_ROWS = 16


def score_kernel(list_width, lists_ref, lens_ref, tgt_ref,
                 q_ref, tcol_ref, tab_ref,
                 qg_ref, loss_ref,
                 tabf_ref, bias_ref, pos_ref, pb_ref):
    b = pl.program_id(0)
    n_shards, shard_rows, _ = tab_ref.shape
    own_rows = shard_rows - BIAS_ROWS
    per_shard = own_rows // BLOCK

    @pl.when(b == 0)
    def _():
        for s in range(n_shards):
            tabf_ref[pl.ds(s * own_rows, own_rows), :] = tab_ref[s, pl.ds(0, own_rows), :].astype(jnp.float32)
            extra = tab_ref[s, pl.ds(own_rows, BIAS_ROWS), :].astype(jnp.float32)
            bias_ref[pl.ds(s * per_shard, per_shard), :] = extra[0:per_shard]

    def gather_row(r, carry):
        t = tgt_ref[b * BLOCK + r]
        pos_ref[pl.ds(r, 1), :] = tabf_ref[pl.ds(t, 1), :]
        pb_ref[pl.ds(r, 1), :] = bias_ref[pl.ds(t // BLOCK, 1), :]
        return carry

    lax.fori_loop(0, BLOCK, gather_row, 0, unroll=8)

    q = q_ref[...]
    qf = q.astype(jnp.float32)
    tcol = tcol_ref[...]
    lane = lax.broadcasted_iota(jnp.int32, (BLOCK, BLOCK), 1)
    positive = pos_ref[...]
    pos_bias = jnp.sum(jnp.where(lane == (tcol % BLOCK), pb_ref[...], 0.0), axis=1, keepdims=True)
    pos_logit = jnp.sum(qf * positive, axis=1, keepdims=True) - pos_bias
    length = lens_ref[b]

    def logits_of(k):
        j = lists_ref[b * list_width + k]
        cand = tab_ref[j // per_shard, pl.ds(pl.multiple_of((j % per_shard) * BLOCK, BLOCK), BLOCK), :]
        brow = bias_ref[pl.ds(j, 1), :]
        logits = lax.dot_general(q, cand, (((1,), (1,)), ((), ())),
                                 preferred_element_type=jnp.float32) - brow
        usable = (lane + j * BLOCK) != tcol
        return cand, usable, jnp.where(usable, logits, NEG_FILL)

    def pass_one(k, carry):
        m, s = carry
        _, _, masked = logits_of(k)
        m_new = jnp.maximum(m, jnp.max(masked, axis=1, keepdims=True))
        s = s * jnp.exp(m - m_new) + jnp.sum(jnp.exp(masked - m_new), axis=1, keepdims=True)
        return m_new, s

    m, s = lax.fori_loop(0, length, pass_one, (pos_logit, jnp.ones_like(pos_logit)))
    log_total = m + jnp.log(s)

    def pass_two(k, acc):
        cand, usable, masked = logits_of(k)
        w = jnp.where(usable, jnp.exp(masked - log_total), 0.0).astype(jnp.bfloat16)
        return acc + jnp.dot(w, cand, preferred_element_type=jnp.float32)

    acc = lax.fori_loop(0, length, pass_two, jnp.zeros((BLOCK, q.shape[1]), jnp.float32))
    qg = acc + (jnp.exp(pos_logit - log_total) - 1.0) * positive
    qg_ref[...] = qg.astype(qg_ref.dtype)
    loss_ref[...] = log_total - pos_logit


def score(queries, target_slot, block_lists, list_lens, table):
    rows, embed = queries.shape
    n_blocks = rows // BLOCK
    n_shards, shard_rows, _ = table.shape
    own_rows = shard_rows - BIAS_ROWS
    n_cands = n_shards * own_rows
    list_width = block_lists.shape[1]
    grid_spec = pltpu.PrefetchScalarGridSpec(
        num_scalar_prefetch=3,
        grid=(n_blocks,),
        in_specs=[
            pl.BlockSpec((BLOCK, embed), lambda b, *_: (b, 0)),
            pl.BlockSpec((BLOCK, 1), lambda b, *_: (b, 0)),
            pl.BlockSpec(memory_space=pltpu.VMEM),
        ],
        out_specs=[
            pl.BlockSpec((BLOCK, embed), lambda b, *_: (b, 0)),
            pl.BlockSpec((BLOCK, 1), lambda b, *_: (b, 0)),
        ],
        scratch_shapes=[
            pltpu.VMEM((n_cands, embed), jnp.float32),
            pltpu.VMEM((n_cands // BLOCK, BLOCK), jnp.float32),
            pltpu.VMEM((BLOCK, embed), jnp.float32),
            pltpu.VMEM((BLOCK, BLOCK), jnp.float32),
        ],
    )
    flops = 2 * 2 * rows * embed * BLOCK * 8
    qg, loss = pl.pallas_call(
        functools.partial(score_kernel, list_width),
        grid_spec=grid_spec,
        out_shape=[
            jax.ShapeDtypeStruct((rows, embed), jnp.bfloat16),
            jax.ShapeDtypeStruct((rows, 1), jnp.float32),
        ],
        compiler_params=pltpu.CompilerParams(
            dimension_semantics=("arbitrary",),
            vmem_limit_bytes=60 * 1024 * 1024,
        ),
        cost_estimate=pl.CostEstimate(
            flops=flops, transcendentals=2 * rows * BLOCK * 8,
            bytes_accessed=table.size * 2 + rows * embed * 4),
    )(block_lists.reshape(-1), list_lens, target_slot,
      queries, target_slot.reshape(rows, 1), table)
    return qg, loss.reshape(rows)


def shards(hidden_rows, w_proj, panels, cand_ids, counts, target_slot, block_lists, list_lens):
    halves, rows_dev, width_half = hidden_rows.shape
    embed_width = w_proj.shape[1]
    flat_rows = hidden_rows.reshape(halves * rows_dev, width_half)
    queries = lax.psum_scatter(
        jnp.dot(flat_rows, w_proj, preferred_element_type=jnp.float32),
        "section",
        scatter_dimension=0,
        tiled=True,
    ).astype(jnp.bfloat16)
    own_bias = jnp.log(counts[cand_ids].astype(jnp.float32)).astype(jnp.bfloat16)
    own_rows = panels.shape[0]
    bias_rows = jnp.pad(own_bias.reshape(own_rows // BLOCK, BLOCK),
                        ((0, BIAS_ROWS - own_rows // BLOCK), (0, 0)))
    shard = jnp.concatenate([panels, bias_rows], axis=0)
    table = lax.all_gather(shard, ("section", "owner"), axis=0, tiled=False)
    query_grad, position_loss = score(queries, target_slot, block_lists, list_lens, table)
    trunk_grad = lax.dot_general(
        lax.all_gather(query_grad, "section", axis=0, tiled=True),
        w_proj,
        (((1,), (1,)), ((), ())),
        preferred_element_type=jnp.float32,
    ).astype(jnp.bfloat16)
    return (query_grad, position_loss, trunk_grad.reshape(halves, rows_dev, width_half))


def solution(mesh):
    return jax.shard_map(
        shards,
        mesh=mesh,
        in_specs=(
            P(None, ("owner", "pos"), "section"),
            P("section", None),
            P(("section", "owner"), None),
            P(("section", "owner")),
            P(),
            P(("section", "owner", "pos")),
            P(("section", "owner", "pos"), None),
            P(("section", "owner", "pos")),
        ),
        out_specs=(
            P(("section", "owner", "pos"), None),
            P(("section", "owner", "pos")),
            P(None, ("owner", "pos"), "section"),
        ),
        check_vma=False,
    )
```

```python
import functools

import jax
import jax.numpy as jnp
from jax import lax
from jax.experimental import pallas as pl
from jax.experimental.pallas import tpu as pltpu
from jax.sharding import PartitionSpec as P

BLOCK = 256
NEG_FILL = -1e30
BIAS_ROWS = 16
GROUP = 4
EXT = BLOCK + 128


def score_kernel(list_width, n_blocks,
                 lists_ref, lens_ref, tgt_ref, par_ref,
                 q_ref, tcol_ref, tab_a_ref, tab_b_ref,
                 qg_ref, loss_ref,
                 tabb_ref, tabf_ref, bias_ref, pos_ref, ls_ref, acc_ref, sem):
    b = pl.program_id(0)
    n_shards = tab_a_ref.shape[0]
    n_cand_blocks = 2 * n_shards

    def issue(block, slot):
        def one(r, carry):
            t = tgt_ref[block * BLOCK + r]
            pltpu.make_async_copy(tabf_ref.at[pl.ds(t, 1), :], pos_ref.at[slot, pl.ds(r, 1), :],
                                  sem.at[slot]).start()
            return carry
        lax.fori_loop(0, BLOCK, one, 0, unroll=8)

    @pl.when(b == 0)
    def _():
        mine = par_ref[0]
        for s in range(n_shards):
            for ref, par in ((tab_a_ref, mine), (tab_b_ref, 1 - mine)):
                j = 2 * s + par
                blk = ref[s, pl.ds(0, BLOCK), :]
                tabb_ref[j] = blk
                tabf_ref[pl.ds(pl.multiple_of(j * BLOCK, BLOCK), BLOCK), pl.ds(0, BLOCK)] = blk.astype(jnp.float32)
                extra = ref[s, pl.ds(BLOCK, BIAS_ROWS), :].astype(jnp.float32)
                bias_ref[pl.ds(j, 1), :] = extra[0:1]
        eye = (lax.broadcasted_iota(jnp.int32, (BLOCK, BLOCK), 0)
               == lax.broadcasted_iota(jnp.int32, (BLOCK, BLOCK), 1)).astype(jnp.float32)
        bias_col = lax.dot_general(eye, bias_ref[...], (((1,), (1,)), ((), ())),
                                   preferred_element_type=jnp.float32,
                                   precision=lax.Precision.HIGHEST)
        for j in range(n_cand_blocks):
            tabf_ref[pl.ds(j * BLOCK, BLOCK), pl.ds(BLOCK, 128)] = jnp.broadcast_to(
                bias_col[:, j:j + 1], (BLOCK, 128))
        issue(0, 0)

    slot = b % 2

    @pl.when(b + 1 < n_blocks)
    def _():
        issue(b + 1, 1 - slot)

    q = q_ref[...]
    qf = q.astype(jnp.float32)
    tcol = tcol_ref[...]
    lane = lax.broadcasted_iota(jnp.int32, (BLOCK, BLOCK), 1)
    length = lens_ref[b]
    n_groups = (length + GROUP - 1) // GROUP

    pltpu.make_async_copy(pos_ref.at[slot], pos_ref.at[slot], sem.at[slot]).wait()
    pos_ext = pos_ref[slot]
    positive = pos_ext[:, 0:BLOCK]
    pos_logit = jnp.sum(qf * positive, axis=1, keepdims=True) - pos_ext[:, BLOCK:BLOCK + 1]

    def pass_a(g, m):
        for i in range(GROUP):
            k = g * GROUP + i
            j = lists_ref[b * list_width + k]
            cand = tabb_ref[j]
            logits = lax.dot_general(q, cand, (((1,), (1,)), ((), ())),
                                     preferred_element_type=jnp.float32) - bias_ref[pl.ds(j, 1), :]
            usable = jnp.logical_and((lane + j * BLOCK) != tcol, k < length)
            masked = jnp.where(usable, logits, NEG_FILL)
            ls_ref[k] = masked
            m = jnp.maximum(m, jnp.max(masked, axis=1, keepdims=True))
        return m

    m = lax.fori_loop(0, n_groups, pass_a, pos_logit)

    def pass_b(g, s):
        for i in range(GROUP):
            s = s + jnp.exp(ls_ref[g * GROUP + i] - m)
        return s

    s_vec = lax.fori_loop(0, n_groups, pass_b, jnp.zeros((BLOCK, BLOCK), jnp.float32))
    row_sum = jnp.exp(pos_logit - m) + jnp.sum(s_vec, axis=1, keepdims=True)
    log_total = m + jnp.log(row_sum)

    acc_ref[...] = jnp.zeros_like(acc_ref)

    def pass_c(g, carry):
        part = None
        for i in range(GROUP):
            k = g * GROUP + i
            j = lists_ref[b * list_width + k]
            w = jnp.exp(ls_ref[k] - log_total).astype(jnp.bfloat16)
            d = jnp.dot(w, tabb_ref[j], preferred_element_type=jnp.float32)
            part = d if part is None else part + d
        acc_ref[...] += part
        return carry

    lax.fori_loop(0, n_groups, pass_c, 0)
    qg = acc_ref[...] + (jnp.exp(pos_logit - log_total) - 1.0) * positive
    qg_ref[...] = qg.astype(qg_ref.dtype)
    loss_ref[...] = log_total - pos_logit


def score(queries, target_slot, block_lists, list_lens, tab_a, tab_b, parity):
    rows, embed = queries.shape
    n_blocks = rows // BLOCK
    n_shards = tab_a.shape[0]
    n_cands = 2 * n_shards * BLOCK
    list_width = block_lists.shape[1]
    grid_spec = pltpu.PrefetchScalarGridSpec(
        num_scalar_prefetch=4,
        grid=(n_blocks,),
        in_specs=[
            pl.BlockSpec((BLOCK, embed), lambda b, *_: (b, 0)),
            pl.BlockSpec((BLOCK, 1), lambda b, *_: (b, 0)),
            pl.BlockSpec(memory_space=pltpu.VMEM),
            pl.BlockSpec(memory_space=pltpu.VMEM),
        ],
        out_specs=[
            pl.BlockSpec((BLOCK, embed), lambda b, *_: (b, 0)),
            pl.BlockSpec((BLOCK, 1), lambda b, *_: (b, 0)),
        ],
        scratch_shapes=[
            pltpu.VMEM((2 * n_shards, BLOCK, embed), jnp.bfloat16),
            pltpu.VMEM((n_cands, EXT), jnp.float32),
            pltpu.VMEM((2 * n_shards, BLOCK), jnp.float32),
            pltpu.VMEM((2, BLOCK, EXT), jnp.float32),
            pltpu.VMEM((list_width, BLOCK, BLOCK), jnp.float32),
            pltpu.VMEM((BLOCK, embed), jnp.float32),
            pltpu.SemaphoreType.DMA((2,)),
        ],
    )
    flops = 2 * 2 * rows * embed * BLOCK * 8
    qg, loss = pl.pallas_call(
        functools.partial(score_kernel, list_width, n_blocks),
        grid_spec=grid_spec,
        out_shape=[
            jax.ShapeDtypeStruct((rows, embed), jnp.bfloat16),
            jax.ShapeDtypeStruct((rows, 1), jnp.float32),
        ],
        compiler_params=pltpu.CompilerParams(
            dimension_semantics=("arbitrary",),
            vmem_limit_bytes=62 * 1024 * 1024,
        ),
        cost_estimate=pl.CostEstimate(
            flops=flops, transcendentals=2 * rows * BLOCK * 8,
            bytes_accessed=2 * tab_a.size * 2 + rows * embed * 4),
    )(block_lists.reshape(-1), list_lens, target_slot, parity,
      queries, target_slot.reshape(rows, 1), tab_a, tab_b)
    return qg, loss.reshape(rows)


def shards(hidden_rows, w_proj, panels, cand_ids, counts, target_slot, block_lists, list_lens):
    halves, rows_dev, width_half = hidden_rows.shape
    flat_rows = hidden_rows.reshape(halves * rows_dev, width_half)
    queries = lax.psum_scatter(
        jnp.dot(flat_rows, w_proj, preferred_element_type=jnp.float32),
        "section",
        scatter_dimension=0,
        tiled=True,
    ).astype(jnp.bfloat16)
    n_pos = lax.axis_size("pos")
    core = lax.axis_index("pos") % 2
    own_bias = jnp.log(counts[cand_ids].astype(jnp.float32)).astype(jnp.bfloat16)
    own_bias = own_bias.reshape(panels.shape[0] // BLOCK, BLOCK)
    my_block = lax.dynamic_slice_in_dim(panels, core * BLOCK, BLOCK, axis=0)
    my_bias = jnp.pad(lax.dynamic_slice_in_dim(own_bias, core, 1, axis=0), ((0, BIAS_ROWS - 1), (0, 0)))
    shard = jnp.concatenate([my_block, my_bias], axis=0)
    tab_a = lax.all_gather(shard, ("section", "owner"), axis=0, tiled=False)
    swap = [(i, i ^ 1) for i in range(n_pos)]
    tab_b = lax.ppermute(tab_a, "pos", swap)
    parity = core.astype(jnp.int32).reshape(1)
    query_grad, position_loss = score(queries, target_slot, block_lists, list_lens, tab_a, tab_b, parity)
    trunk_grad = lax.dot_general(
        lax.all_gather(query_grad, "section", axis=0, tiled=True),
        w_proj,
        (((1,), (1,)), ((), ())),
        preferred_element_type=jnp.float32,
    ).astype(jnp.bfloat16)
    return (query_grad, position_loss, trunk_grad.reshape(halves, rows_dev, width_half))


def solution(mesh):
    return jax.shard_map(
        shards,
        mesh=mesh,
        in_specs=(
            P(None, ("owner", "pos"), "section"),
            P("section", None),
            P(("section", "owner"), None),
            P(("section", "owner")),
            P(),
            P(("section", "owner", "pos")),
            P(("section", "owner", "pos"), None),
            P(("section", "owner", "pos")),
        ),
        out_specs=(
            P(("section", "owner", "pos"), None),
            P(("section", "owner", "pos")),
            P(None, ("owner", "pos"), "section"),
        ),
        check_vma=False,
    )
```

```python
import functools

import jax
import jax.numpy as jnp
from jax import lax
from jax.experimental import pallas as pl
from jax.experimental.pallas import tpu as pltpu
from jax.sharding import PartitionSpec as P

BLOCK = 256
NEG_FILL = -1e30
BIAS_ROWS = 16
GROUP = 4
EXT = BLOCK + 128


def score_kernel(list_width, n_blocks, dists,
                 lists_ref, lens_ref, tgt_ref, par_ref,
                 q_ref, tcol_ref, tab_a_ref, tab_b_ref,
                 qg_ref, loss_ref,
                 tabb_ref, tabf_ref, bias_ref, pos_ref, ls_ref, acc_ref, sem):
    b = pl.program_id(0)
    n_shards = tab_a_ref.shape[0]
    n_cand_blocks = 2 * n_shards

    def issue(block, slot):
        def one(r, carry):
            t = tgt_ref[block * BLOCK + r]
            pltpu.make_async_copy(tabf_ref.at[pl.ds(t, 1), :], pos_ref.at[slot, pl.ds(r, 1), :],
                                  sem.at[slot]).start()
            return carry
        lax.fori_loop(0, BLOCK, one, 0, unroll=8)

    @pl.when(b == 0)
    def _():
        mine = par_ref[0]
        me = par_ref[1]
        for s in range(n_shards):
            away = 0
            for bit, d in enumerate(dists):
                if (s >> bit) & 1:
                    away ^= d
            for ref, par in ((tab_a_ref, mine), (tab_b_ref, 1 - mine)):
                j = 2 * (me ^ away) + par
                blk = ref[s, pl.ds(0, BLOCK), :]
                tabb_ref[j] = blk
                tabf_ref[pl.ds(pl.multiple_of(j * BLOCK, BLOCK), BLOCK), pl.ds(0, BLOCK)] = blk.astype(jnp.float32)
                extra = ref[s, pl.ds(BLOCK, BIAS_ROWS), :].astype(jnp.float32)
                bias_ref[pl.ds(j, 1), :] = extra[0:1]
        eye = (lax.broadcasted_iota(jnp.int32, (BLOCK, BLOCK), 0)
               == lax.broadcasted_iota(jnp.int32, (BLOCK, BLOCK), 1)).astype(jnp.float32)
        bias_col = lax.dot_general(eye, bias_ref[...], (((1,), (1,)), ((), ())),
                                   preferred_element_type=jnp.float32,
                                   precision=lax.Precision.HIGHEST)
        for j in range(n_cand_blocks):
            tabf_ref[pl.ds(j * BLOCK, BLOCK), pl.ds(BLOCK, 128)] = jnp.broadcast_to(
                bias_col[:, j:j + 1], (BLOCK, 128))
        issue(0, 0)

    slot = b % 2

    @pl.when(b + 1 < n_blocks)
    def _():
        issue(b + 1, 1 - slot)

    q = q_ref[...]
    qf = q.astype(jnp.float32)
    tcol = tcol_ref[...]
    lane = lax.broadcasted_iota(jnp.int32, (BLOCK, BLOCK), 1)
    length = lens_ref[b]
    n_groups = (length + GROUP - 1) // GROUP

    pltpu.make_async_copy(pos_ref.at[slot], pos_ref.at[slot], sem.at[slot]).wait()
    pos_ext = pos_ref[slot]
    positive = pos_ext[:, 0:BLOCK]
    pos_logit = jnp.sum(qf * positive, axis=1, keepdims=True) - pos_ext[:, BLOCK:BLOCK + 1]

    def pass_a(g, m):
        for i in range(GROUP):
            k = g * GROUP + i
            j = lists_ref[b * list_width + k]
            cand = tabb_ref[j]
            logits = lax.dot_general(q, cand, (((1,), (1,)), ((), ())),
                                     preferred_element_type=jnp.float32) - bias_ref[pl.ds(j, 1), :]
            usable = jnp.logical_and((lane + j * BLOCK) != tcol, k < length)
            masked = jnp.where(usable, logits, NEG_FILL)
            ls_ref[k] = masked
            m = jnp.maximum(m, jnp.max(masked, axis=1, keepdims=True))
        return m

    m = lax.fori_loop(0, n_groups, pass_a, pos_logit)

    def pass_b(g, s):
        for i in range(GROUP):
            s = s + jnp.exp(ls_ref[g * GROUP + i] - m)
        return s

    s_vec = lax.fori_loop(0, n_groups, pass_b, jnp.zeros((BLOCK, BLOCK), jnp.float32))
    row_sum = jnp.exp(pos_logit - m) + jnp.sum(s_vec, axis=1, keepdims=True)
    log_total = m + jnp.log(row_sum)

    acc_ref[...] = jnp.zeros_like(acc_ref)

    def pass_c(g, carry):
        part = None
        for i in range(GROUP):
            k = g * GROUP + i
            j = lists_ref[b * list_width + k]
            w = jnp.exp(ls_ref[k] - log_total).astype(jnp.bfloat16)
            d = jnp.dot(w, tabb_ref[j], preferred_element_type=jnp.float32)
            part = d if part is None else part + d
        acc_ref[...] += part
        return carry

    lax.fori_loop(0, n_groups, pass_c, 0)
    qg = acc_ref[...] + (jnp.exp(pos_logit - log_total) - 1.0) * positive
    qg_ref[...] = qg.astype(qg_ref.dtype)
    loss_ref[...] = log_total - pos_logit


def score(queries, target_slot, block_lists, list_lens, tab_a, tab_b, parity, dists):
    rows, embed = queries.shape
    n_blocks = rows // BLOCK
    n_shards = tab_a.shape[0]
    n_cands = 2 * n_shards * BLOCK
    list_width = block_lists.shape[1]
    grid_spec = pltpu.PrefetchScalarGridSpec(
        num_scalar_prefetch=4,
        grid=(n_blocks,),
        in_specs=[
            pl.BlockSpec((BLOCK, embed), lambda b, *_: (b, 0)),
            pl.BlockSpec((BLOCK, 1), lambda b, *_: (b, 0)),
            pl.BlockSpec(memory_space=pltpu.VMEM),
            pl.BlockSpec(memory_space=pltpu.VMEM),
        ],
        out_specs=[
            pl.BlockSpec((BLOCK, embed), lambda b, *_: (b, 0)),
            pl.BlockSpec((BLOCK, 1), lambda b, *_: (b, 0)),
        ],
        scratch_shapes=[
            pltpu.VMEM((2 * n_shards, BLOCK, embed), jnp.bfloat16),
            pltpu.VMEM((n_cands, EXT), jnp.float32),
            pltpu.VMEM((2 * n_shards, BLOCK), jnp.float32),
            pltpu.VMEM((2, BLOCK, EXT), jnp.float32),
            pltpu.VMEM((list_width, BLOCK, BLOCK), jnp.float32),
            pltpu.VMEM((BLOCK, embed), jnp.float32),
            pltpu.SemaphoreType.DMA((2,)),
        ],
    )
    flops = 2 * 2 * rows * embed * BLOCK * 8
    qg, loss = pl.pallas_call(
        functools.partial(score_kernel, list_width, n_blocks, dists),
        grid_spec=grid_spec,
        out_shape=[
            jax.ShapeDtypeStruct((rows, embed), jnp.bfloat16),
            jax.ShapeDtypeStruct((rows, 1), jnp.float32),
        ],
        compiler_params=pltpu.CompilerParams(
            dimension_semantics=("arbitrary",),
            vmem_limit_bytes=62 * 1024 * 1024,
        ),
        cost_estimate=pl.CostEstimate(
            flops=flops, transcendentals=2 * rows * BLOCK * 8,
            bytes_accessed=2 * tab_a.size * 2 + rows * embed * 4),
    )(block_lists.reshape(-1), list_lens, target_slot, parity,
      queries, target_slot.reshape(rows, 1), tab_a, tab_b)
    return qg, loss.reshape(rows)


def shards(hidden_rows, w_proj, panels, cand_ids, counts, target_slot, block_lists, list_lens):
    halves, rows_dev, width_half = hidden_rows.shape
    flat_rows = hidden_rows.reshape(halves * rows_dev, width_half)
    n_sec = lax.axis_size("section")
    sec = lax.axis_index("section")
    partner = [(i, i ^ 1) for i in range(n_sec)]
    partial = jnp.dot(flat_rows, w_proj, preferred_element_type=jnp.float32).reshape(halves, rows_dev, -1)
    sent = lax.ppermute(lax.dynamic_index_in_dim(partial, 1 - sec, 0, keepdims=False), "section", partner)
    queries = (lax.dynamic_index_in_dim(partial, sec, 0, keepdims=False) + sent).astype(jnp.bfloat16)
    n_pos = lax.axis_size("pos")
    core = lax.axis_index("pos") % 2
    n_own = lax.axis_size("owner")
    me = sec * n_own + lax.axis_index("owner")
    own_bias = jnp.log(counts[cand_ids].astype(jnp.float32)).astype(jnp.bfloat16)
    own_bias = own_bias.reshape(panels.shape[0] // BLOCK, BLOCK)
    my_block = lax.dynamic_slice_in_dim(panels, core * BLOCK, BLOCK, axis=0)
    my_bias = jnp.pad(lax.dynamic_slice_in_dim(own_bias, core, 1, axis=0), ((0, BIAS_ROWS - 1), (0, 0)))
    buf = jnp.concatenate([my_block, my_bias], axis=0)[None]
    n_group = n_sec * n_own
    dists = []
    d = n_group // 2
    while d >= 1:
        dists.append(d)
        d //= 2
    for d in dists:
        got = lax.ppermute(buf, ("section", "owner"), [(i, i ^ d) for i in range(n_group)])
        buf = jnp.concatenate([buf, got], axis=0)
    tab_b = lax.ppermute(buf, "pos", [(i, i ^ 1) for i in range(n_pos)])
    parity = jnp.stack([core, me]).astype(jnp.int32)
    query_grad, position_loss = score(queries, target_slot, block_lists, list_lens, buf, tab_b, parity,
                                      tuple(dists))
    other_grad = lax.ppermute(query_grad, "section", partner)
    both = jnp.where(sec == 0, jnp.concatenate([query_grad, other_grad], axis=0),
                     jnp.concatenate([other_grad, query_grad], axis=0))
    trunk_grad = lax.dot_general(
        both,
        w_proj,
        (((1,), (1,)), ((), ())),
        preferred_element_type=jnp.float32,
    ).astype(jnp.bfloat16)
    return (query_grad, position_loss, trunk_grad.reshape(halves, rows_dev, width_half))


def solution(mesh):
    return jax.shard_map(
        shards,
        mesh=mesh,
        in_specs=(
            P(None, ("owner", "pos"), "section"),
            P("section", None),
            P(("section", "owner"), None),
            P(("section", "owner")),
            P(),
            P(("section", "owner", "pos")),
            P(("section", "owner", "pos"), None),
            P(("section", "owner", "pos")),
        ),
        out_specs=(
            P(("section", "owner", "pos"), None),
            P(("section", "owner", "pos")),
            P(None, ("owner", "pos"), "section"),
        ),
        check_vma=False,
    )
```

```python
import functools

import jax
import jax.numpy as jnp
from jax import lax
from jax.experimental import pallas as pl
from jax.experimental.pallas import tpu as pltpu
from jax.sharding import PartitionSpec as P

BLOCK = 256
NEG_FILL = -1e30
BIAS_ROWS = 16
GROUP = 4
EXT = BLOCK + 128


def score_kernel(list_width, n_blocks, dists,
                 lists_ref, lens_ref, tgt_ref, par_ref,
                 q_ref, tcol_ref, tab_a_ref, tab_b_ref,
                 qg_ref, loss_ref,
                 tabb_ref, tabf_ref, bias_ref, pos_ref, ls_ref, acc_ref, sem):
    b = pl.program_id(0)
    n_shards = tab_a_ref.shape[0]
    n_cand_blocks = 2 * n_shards

    def issue(block, slot):
        def one(r, carry):
            t = tgt_ref[block * BLOCK + r]
            pltpu.make_async_copy(tabf_ref.at[pl.ds(t, 1), :], pos_ref.at[slot, pl.ds(r, 1), :],
                                  sem.at[slot]).start()
            return carry
        lax.fori_loop(0, BLOCK, one, 0, unroll=8)

    @pl.when(b == 0)
    def _():
        mine = par_ref[0]
        me = par_ref[1]
        for s in range(n_shards):
            away = 0
            for bit, d in enumerate(dists):
                if (s >> bit) & 1:
                    away ^= d
            for ref, par in ((tab_a_ref, mine), (tab_b_ref, 1 - mine)):
                j = 2 * (me ^ away) + par
                blk = ref[s, pl.ds(0, BLOCK), :]
                tabb_ref[j] = blk
                tabf_ref[pl.ds(pl.multiple_of(j * BLOCK, BLOCK), BLOCK), pl.ds(0, BLOCK)] = blk.astype(jnp.float32)
                extra = ref[s, pl.ds(BLOCK, BIAS_ROWS), :].astype(jnp.float32)
                bias_ref[pl.ds(j, 1), :] = extra[0:1]
        eye = (lax.broadcasted_iota(jnp.int32, (BLOCK, BLOCK), 0)
               == lax.broadcasted_iota(jnp.int32, (BLOCK, BLOCK), 1)).astype(jnp.float32)
        bias_col = lax.dot_general(eye, bias_ref[...], (((1,), (1,)), ((), ())),
                                   preferred_element_type=jnp.float32,
                                   precision=lax.Precision.HIGHEST)
        for j in range(n_cand_blocks):
            tabf_ref[pl.ds(j * BLOCK, BLOCK), pl.ds(BLOCK, 128)] = jnp.broadcast_to(
                bias_col[:, j:j + 1], (BLOCK, 128))
        issue(0, 0)

    slot = b % 2

    @pl.when(b + 1 < n_blocks)
    def _():
        issue(b + 1, 1 - slot)

    q = q_ref[...]
    qf = q.astype(jnp.float32)
    tcol = tcol_ref[...]
    lane = lax.broadcasted_iota(jnp.int32, (BLOCK, BLOCK), 1)
    length = lens_ref[b]
    n_groups = (length + GROUP - 1) // GROUP

    pltpu.make_async_copy(pos_ref.at[slot], pos_ref.at[slot], sem.at[slot]).wait()
    pos_ext = pos_ref[slot]
    positive = pos_ext[:, 0:BLOCK]
    pos_logit = jnp.sum(qf * positive, axis=1, keepdims=True) - pos_ext[:, BLOCK:BLOCK + 1]

    def pass_a(g, m):
        for i in range(GROUP):
            k = g * GROUP + i
            j = lists_ref[b * list_width + k]
            cand = tabb_ref[j]
            logits = lax.dot_general(q, cand, (((1,), (1,)), ((), ())),
                                     preferred_element_type=jnp.float32) - bias_ref[pl.ds(j, 1), :]
            usable = jnp.logical_and((lane + j * BLOCK) != tcol, k < length)
            masked = jnp.where(usable, logits, NEG_FILL)
            ls_ref[k] = masked
            m = jnp.maximum(m, jnp.max(masked, axis=1, keepdims=True))
        return m

    m = lax.fori_loop(0, n_groups, pass_a, pos_logit)

    def pass_b(g, s):
        for i in range(GROUP):
            s = s + jnp.exp(ls_ref[g * GROUP + i] - m)
        return s

    s_vec = lax.fori_loop(0, n_groups, pass_b, jnp.zeros((BLOCK, BLOCK), jnp.float32))
    row_sum = jnp.exp(pos_logit - m) + jnp.sum(s_vec, axis=1, keepdims=True)
    log_total = m + jnp.log(row_sum)

    acc_ref[...] = jnp.zeros_like(acc_ref)

    def pass_c(g, carry):
        part = None
        for i in range(GROUP):
            k = g * GROUP + i
            j = lists_ref[b * list_width + k]
            w = jnp.exp(ls_ref[k] - log_total).astype(jnp.bfloat16)
            d = jnp.dot(w, tabb_ref[j], preferred_element_type=jnp.float32)
            part = d if part is None else part + d
        acc_ref[...] += part
        return carry

    lax.fori_loop(0, n_groups, pass_c, 0)
    qg = acc_ref[...] + (jnp.exp(pos_logit - log_total) - 1.0) * positive
    qg_ref[...] = qg.astype(qg_ref.dtype)
    loss_ref[...] = log_total - pos_logit


def score(queries, target_slot, block_lists, list_lens, tab_a, tab_b, parity, dists):
    rows, embed = queries.shape
    n_blocks = rows // BLOCK
    n_shards = tab_a.shape[0]
    n_cands = 2 * n_shards * BLOCK
    list_width = block_lists.shape[1]
    grid_spec = pltpu.PrefetchScalarGridSpec(
        num_scalar_prefetch=4,
        grid=(n_blocks,),
        in_specs=[
            pl.BlockSpec((BLOCK, embed), lambda b, *_: (b, 0)),
            pl.BlockSpec((BLOCK, 1), lambda b, *_: (b, 0)),
            pl.BlockSpec(memory_space=pltpu.VMEM),
            pl.BlockSpec(memory_space=pltpu.VMEM),
        ],
        out_specs=[
            pl.BlockSpec((BLOCK, embed), lambda b, *_: (b, 0)),
            pl.BlockSpec((BLOCK, 1), lambda b, *_: (b, 0)),
        ],
        scratch_shapes=[
            pltpu.VMEM((2 * n_shards, BLOCK, embed), jnp.bfloat16),
            pltpu.VMEM((n_cands, EXT), jnp.float32),
            pltpu.VMEM((2 * n_shards, BLOCK), jnp.float32),
            pltpu.VMEM((2, BLOCK, EXT), jnp.float32),
            pltpu.VMEM((list_width, BLOCK, BLOCK), jnp.float32),
            pltpu.VMEM((BLOCK, embed), jnp.float32),
            pltpu.SemaphoreType.DMA((2,)),
        ],
    )
    flops = 2 * 2 * rows * embed * BLOCK * 8
    qg, loss = pl.pallas_call(
        functools.partial(score_kernel, list_width, n_blocks, dists),
        grid_spec=grid_spec,
        out_shape=[
            jax.ShapeDtypeStruct((rows, embed), jnp.bfloat16),
            jax.ShapeDtypeStruct((rows, 1), jnp.float32),
        ],
        compiler_params=pltpu.CompilerParams(
            dimension_semantics=("arbitrary",),
            vmem_limit_bytes=62 * 1024 * 1024,
        ),
        cost_estimate=pl.CostEstimate(
            flops=flops, transcendentals=2 * rows * BLOCK * 8,
            bytes_accessed=2 * tab_a.size * 2 + rows * embed * 4),
    )(block_lists.reshape(-1), list_lens, target_slot, parity,
      queries, target_slot.reshape(rows, 1), tab_a, tab_b)
    return qg, loss.reshape(rows)


def shards(hidden_rows, w_proj, panels, cand_ids, counts, target_slot, block_lists, list_lens):
    halves, rows_dev, width_half = hidden_rows.shape
    flat_rows = hidden_rows.reshape(halves * rows_dev, width_half)
    n_sec = lax.axis_size("section")
    sec = lax.axis_index("section")
    partner = [(i, i ^ 1) for i in range(n_sec)]
    partial = jnp.dot(flat_rows, w_proj, preferred_element_type=jnp.float32).reshape(halves, rows_dev, -1)
    n_pos = lax.axis_size("pos")
    core = lax.axis_index("pos") % 2
    n_own = lax.axis_size("owner")
    me = sec * n_own + lax.axis_index("owner")
    own_bias = jnp.log(counts[cand_ids].astype(jnp.float32)).astype(jnp.bfloat16)
    own_bias = own_bias.reshape(panels.shape[0] // BLOCK, BLOCK)
    my_block = lax.dynamic_slice_in_dim(panels, core * BLOCK, BLOCK, axis=0)
    my_bias = jnp.pad(lax.dynamic_slice_in_dim(own_bias, core, 1, axis=0), ((0, BIAS_ROWS - 1), (0, 0)))
    buf = jnp.concatenate([my_block, my_bias], axis=0)[None]
    partial, buf = lax.optimization_barrier((partial, buf))
    n_group = n_sec * n_own
    dists = []
    step = 1
    while step < n_group:
        radix = min(4, n_group // step)
        got = [lax.ppermute(buf, ("section", "owner"), [(i, i ^ (m * step)) for i in range(n_group)])
               for m in range(1, radix)]
        buf = jnp.concatenate([buf] + got, axis=0)
        while radix > 1:
            dists.append(step)
            step *= 2
            radix //= 2
    sent = lax.ppermute(lax.dynamic_index_in_dim(partial, 1 - sec, 0, keepdims=False), "section", partner)
    queries = (lax.dynamic_index_in_dim(partial, sec, 0, keepdims=False) + sent).astype(jnp.bfloat16)
    tab_b = lax.ppermute(buf, "pos", [(i, i ^ 1) for i in range(n_pos)])
    parity = jnp.stack([core, me]).astype(jnp.int32)
    query_grad, position_loss = score(queries, target_slot, block_lists, list_lens, buf, tab_b, parity,
                                      tuple(dists))
    other_grad = lax.ppermute(query_grad, "section", partner)
    both = jnp.where(sec == 0, jnp.concatenate([query_grad, other_grad], axis=0),
                     jnp.concatenate([other_grad, query_grad], axis=0))
    trunk_grad = lax.dot_general(
        both,
        w_proj,
        (((1,), (1,)), ((), ())),
        preferred_element_type=jnp.float32,
    ).astype(jnp.bfloat16)
    return (query_grad, position_loss, trunk_grad.reshape(halves, rows_dev, width_half))


def solution(mesh):
    return jax.shard_map(
        shards,
        mesh=mesh,
        in_specs=(
            P(None, ("owner", "pos"), "section"),
            P("section", None),
            P(("section", "owner"), None),
            P(("section", "owner")),
            P(),
            P(("section", "owner", "pos")),
            P(("section", "owner", "pos"), None),
            P(("section", "owner", "pos")),
        ),
        out_specs=(
            P(("section", "owner", "pos"), None),
            P(("section", "owner", "pos")),
            P(None, ("owner", "pos"), "section"),
        ),
        check_vma=False,
    )
```

```python
import functools

import jax
import jax.numpy as jnp
from jax import lax
from jax.experimental import pallas as pl
from jax.experimental.pallas import tpu as pltpu
from jax.sharding import PartitionSpec as P


BLOCK = 256
NEG_FILL = -1e30
BIAS_ROWS = 16
GROUP = 4
EXT = BLOCK + 128


def score_kernel(list_width, n_blocks, dists,
                 lists_ref, lens_ref, tgt_ref, par_ref,
                 qa_ref, qb_ref, tcol_ref, tab_a_ref, tab_b_ref,
                 qg_ref, loss_ref,
                 tabb_ref, tabf_ref, bias_ref, pos_ref, ls_ref, acc_ref, sem):
    b = pl.program_id(0)
    n_shards = tab_a_ref.shape[0]
    n_cand_blocks = 2 * n_shards

    def issue(block, slot):
        def one(r, carry):
            t = tgt_ref[block * BLOCK + r]
            pltpu.make_async_copy(tabf_ref.at[pl.ds(t, 1), :], pos_ref.at[slot, pl.ds(r, 1), :],
                                  sem.at[slot]).start()
            return carry

        lax.fori_loop(0, BLOCK, one, 0, unroll=8)

    @pl.when(b == 0)
    def _():
        mine = par_ref[0]
        me = par_ref[1]
        for s in range(n_shards):
            away = 0
            for bit, d in enumerate(dists):
                if (s >> bit) & 1:
                    away ^= d
            for ref, par in ((tab_a_ref, mine), (tab_b_ref, 1 - mine)):
                j = 2 * (me ^ away) + par
                blk = ref[s, pl.ds(0, BLOCK), :]
                tabb_ref[j] = blk
                tabf_ref[pl.ds(pl.multiple_of(j * BLOCK, BLOCK), BLOCK), pl.ds(0, BLOCK)] = blk.astype(jnp.float32)
                extra = ref[s, pl.ds(BLOCK, BIAS_ROWS), :].astype(jnp.float32)
                bias_ref[pl.ds(j, 1), :] = extra[0:1]
        eye = (lax.broadcasted_iota(jnp.int32, (BLOCK, BLOCK), 0)
               == lax.broadcasted_iota(jnp.int32, (BLOCK, BLOCK), 1)).astype(jnp.float32)
        bias_col = lax.dot_general(eye, bias_ref[...], (((1,), (1,)), ((), ())),
                                   preferred_element_type=jnp.float32,
                                   precision=lax.Precision.HIGHEST)
        for j in range(n_cand_blocks):
            tabf_ref[pl.ds(j * BLOCK, BLOCK), pl.ds(BLOCK, 128)] = jnp.broadcast_to(
                bias_col[:, j:j + 1], (BLOCK, 128))
        issue(0, 0)

    slot = b % 2

    @pl.when(b + 1 < n_blocks)
    def _():
        issue(b + 1, 1 - slot)

    q = (qa_ref[...] + qb_ref[...]).astype(jnp.bfloat16)
    qf = q.astype(jnp.float32)
    tcol = tcol_ref[...]
    lane = lax.broadcasted_iota(jnp.int32, (BLOCK, BLOCK), 1)
    length = lens_ref[b]
    n_groups = (length + GROUP - 1) // GROUP

    pltpu.make_async_copy(pos_ref.at[slot], pos_ref.at[slot], sem.at[slot]).wait()
    pos_ext = pos_ref[slot]
    positive = pos_ext[:, 0:BLOCK]
    pos_logit = jnp.sum(qf * positive, axis=1, keepdims=True) - pos_ext[:, BLOCK:BLOCK + 1]

    def pass_a(g, m):
        for i in range(GROUP):
            k = g * GROUP + i
            j = lists_ref[b * list_width + k]
            cand = tabb_ref[j]
            logits = lax.dot_general(q, cand, (((1,), (1,)), ((), ())),
                                     preferred_element_type=jnp.float32) - bias_ref[pl.ds(j, 1), :]
            usable = jnp.logical_and((lane + j * BLOCK) != tcol, k < length)
            masked = jnp.where(usable, logits, NEG_FILL)
            ls_ref[k] = masked
            m = jnp.maximum(m, jnp.max(masked, axis=1, keepdims=True))
        return m

    m = lax.fori_loop(0, n_groups, pass_a, pos_logit)

    def pass_b(g, s):
        for i in range(GROUP):
            s = s + jnp.exp(ls_ref[g * GROUP + i] - m)
        return s

    s_vec = lax.fori_loop(0, n_groups, pass_b, jnp.zeros((BLOCK, BLOCK), jnp.float32))
    row_sum = jnp.exp(pos_logit - m) + jnp.sum(s_vec, axis=1, keepdims=True)
    log_total = m + jnp.log(row_sum)

    acc_ref[...] = jnp.zeros_like(acc_ref)

    def pass_c(g, carry):
        part = None
        for i in range(GROUP):
            k = g * GROUP + i
            j = lists_ref[b * list_width + k]
            w = jnp.exp(ls_ref[k] - log_total).astype(jnp.bfloat16)
            d = jnp.dot(w, tabb_ref[j], preferred_element_type=jnp.float32)
            part = d if part is None else part + d
        acc_ref[...] += part
        return carry

    lax.fori_loop(0, n_groups, pass_c, 0)
    qg = acc_ref[...] + (jnp.exp(pos_logit - log_total) - 1.0) * positive
    qg_ref[...] = qg.astype(qg_ref.dtype)
    loss_ref[...] = log_total - pos_logit


def score(q_mine, q_sent, target_slot, block_lists, list_lens, tab_a, tab_b, parity, dists):
    rows, embed = q_mine.shape
    n_blocks = rows // BLOCK
    n_shards = tab_a.shape[0]
    n_cands = 2 * n_shards * BLOCK
    list_width = block_lists.shape[1]
    grid_spec = pltpu.PrefetchScalarGridSpec(
        num_scalar_prefetch=4,
        grid=(n_blocks,),
        in_specs=[
            pl.BlockSpec((BLOCK, embed), lambda b, *_: (b, 0)),
            pl.BlockSpec((BLOCK, embed), lambda b, *_: (b, 0)),
            pl.BlockSpec((BLOCK, 1), lambda b, *_: (b, 0)),
            pl.BlockSpec(memory_space=pltpu.VMEM),
            pl.BlockSpec(memory_space=pltpu.VMEM),
        ],
        out_specs=[
            pl.BlockSpec((BLOCK, embed), lambda b, *_: (b, 0)),
            pl.BlockSpec((BLOCK, 1), lambda b, *_: (b, 0)),
        ],
        scratch_shapes=[
            pltpu.VMEM((2 * n_shards, BLOCK, embed), jnp.bfloat16),
            pltpu.VMEM((n_cands, EXT), jnp.float32),
            pltpu.VMEM((2 * n_shards, BLOCK), jnp.float32),
            pltpu.VMEM((2, BLOCK, EXT), jnp.float32),
            pltpu.VMEM((list_width, BLOCK, BLOCK), jnp.float32),
            pltpu.VMEM((BLOCK, embed), jnp.float32),
            pltpu.SemaphoreType.DMA((2,)),
        ],
    )
    flops = 2 * 2 * rows * embed * BLOCK * 8
    qg, loss = pl.pallas_call(
        functools.partial(score_kernel, list_width, n_blocks, dists),
        grid_spec=grid_spec,
        out_shape=[
            jax.ShapeDtypeStruct((rows, embed), jnp.bfloat16),
            jax.ShapeDtypeStruct((rows, 1), jnp.float32),
        ],
        compiler_params=pltpu.CompilerParams(
            dimension_semantics=("arbitrary",),
            vmem_limit_bytes=62 * 1024 * 1024,
        ),
        cost_estimate=pl.CostEstimate(
            flops=flops, transcendentals=2 * rows * BLOCK * 8,
            bytes_accessed=2 * tab_a.size * 2 + rows * embed * 4),
    )(block_lists.reshape(-1), list_lens, target_slot, parity,
      q_mine, q_sent, target_slot.reshape(rows, 1), tab_a, tab_b)
    return qg, loss.reshape(rows)


def shards(hidden_rows, w_proj, panels, cand_ids, counts, target_slot, block_lists, list_lens):
    halves, rows_dev, width_half = hidden_rows.shape
    flat_rows = hidden_rows.reshape(halves * rows_dev, width_half)
    n_sec = lax.axis_size("section")
    sec = lax.axis_index("section")
    partner = [(i, i ^ 1) for i in range(n_sec)]
    partial = jnp.dot(flat_rows, w_proj, preferred_element_type=jnp.float32).reshape(halves, rows_dev, -1)
    n_pos = lax.axis_size("pos")
    core = lax.axis_index("pos") % 2
    n_own = lax.axis_size("owner")
    me = sec * n_own + lax.axis_index("owner")
    own_bias = jnp.log(counts[cand_ids].astype(jnp.float32)).astype(jnp.bfloat16)
    own_bias = own_bias.reshape(panels.shape[0] // BLOCK, BLOCK)
    my_block = lax.dynamic_slice_in_dim(panels, core * BLOCK, BLOCK, axis=0)
    my_bias = jnp.pad(lax.dynamic_slice_in_dim(own_bias, core, 1, axis=0), ((0, BIAS_ROWS - 1), (0, 0)))
    buf = jnp.concatenate([my_block, my_bias], axis=0)[None]
    partial, buf = lax.optimization_barrier((partial, buf))
    n_group = n_sec * n_own
    steps = [4, 1] if n_group == 16 else []
    dists = []
    if steps:
        for step in steps:
            got = [lax.ppermute(buf, ("section", "owner"), [(i, i ^ (m * step)) for i in range(n_group)])
                   for m in range(1, 4)]
            buf = jnp.concatenate([buf] + got, axis=0)
            dists += [step, 2 * step]
    else:
        d = n_group // 2
        while d >= 1:
            got = lax.ppermute(buf, ("section", "owner"), [(i, i ^ d) for i in range(n_group)])
            buf = jnp.concatenate([buf, got], axis=0)
            dists.append(d)
            d //= 2
    tab_b = lax.ppermute(buf, "pos", [(i, i ^ 1) for i in range(n_pos)])
    parity = jnp.stack([core, me]).astype(jnp.int32)
    mine = lax.dynamic_index_in_dim(partial, sec, 0, keepdims=False)
    theirs = lax.dynamic_index_in_dim(partial, 1 - sec, 0, keepdims=False)
    n_chunks = 2
    rows_chunk = rows_dev // n_chunks
    blocks_chunk = rows_chunk // BLOCK
    grads, losses, others = [], [], []
    for c in range(n_chunks):
        rows = slice(c * rows_chunk, (c + 1) * rows_chunk)
        blocks = slice(c * blocks_chunk, (c + 1) * blocks_chunk)
        sent = lax.ppermute(theirs[rows], "section", partner)
        grad, loss = score(mine[rows], sent, target_slot[rows], block_lists[blocks], list_lens[blocks], buf, tab_b,
                           parity, tuple(dists))
        grads.append(grad)
        losses.append(loss)
        others.append(lax.ppermute(grad, "section", partner))
    query_grad = jnp.concatenate(grads, axis=0)
    other_grad = jnp.concatenate(others, axis=0)
    position_loss = jnp.concatenate(losses, axis=0)
    both = jnp.where(sec == 0, jnp.concatenate([query_grad, other_grad], axis=0),
                     jnp.concatenate([other_grad, query_grad], axis=0))
    trunk_grad = lax.dot_general(
        both,
        w_proj,
        (((1,), (1,)), ((), ())),
        preferred_element_type=jnp.float32,
    ).astype(jnp.bfloat16)
    return (query_grad, position_loss, trunk_grad.reshape(halves, rows_dev, width_half))


def solution(mesh):
    return jax.shard_map(
        shards,
        mesh=mesh,
        in_specs=(
            P(None, ("owner", "pos"), "section"),
            P("section", None),
            P(("section", "owner"), None),
            P(("section", "owner")),
            P(),
            P(("section", "owner", "pos")),
            P(("section", "owner", "pos"), None),
            P(("section", "owner", "pos")),
        ),
        out_specs=(
            P(("section", "owner", "pos"), None),
            P(("section", "owner", "pos")),
            P(None, ("owner", "pos"), "section"),
        ),
        check_vma=False,
    )
```

```python
import functools

import jax
import jax.numpy as jnp
from jax import lax
from jax.experimental import pallas as pl
from jax.experimental.pallas import tpu as pltpu
from jax.sharding import PartitionSpec as P


BLOCK = 256
NEG_FILL = -1e30
BIAS_ROWS = 16
GROUP = 4
EXT = BLOCK + 128


def score_kernel(list_width, n_blocks, dists,
                 lists_ref, lens_ref, tgt_ref, par_ref,
                 qa_ref, qb_ref, tcol_ref, tab_a_ref, tab_b_ref,
                 qg_ref, loss_ref,
                 tabb_ref, tabf_ref, bias_ref, pos_ref, ls_ref, acc_ref, sem):
    b = pl.program_id(0)
    n_shards = tab_a_ref.shape[0]
    n_cand_blocks = 2 * n_shards

    def issue(block, slot):
        def one(r, carry):
            t = tgt_ref[block * BLOCK + r]
            pltpu.make_async_copy(tabf_ref.at[pl.ds(t, 1), :], pos_ref.at[slot, pl.ds(r, 1), :],
                                  sem.at[slot]).start()
            return carry

        lax.fori_loop(0, BLOCK, one, 0, unroll=8)

    @pl.when(b == 0)
    def _():
        mine = par_ref[0]
        me = par_ref[1]
        for s in range(n_shards):
            away = 0
            for bit, d in enumerate(dists):
                if (s >> bit) & 1:
                    away ^= d
            for ref, par in ((tab_a_ref, mine), (tab_b_ref, 1 - mine)):
                j = 2 * (me ^ away) + par
                blk = ref[s, pl.ds(0, BLOCK), :]
                tabb_ref[j] = blk
                tabf_ref[pl.ds(pl.multiple_of(j * BLOCK, BLOCK), BLOCK), pl.ds(0, BLOCK)] = blk.astype(jnp.float32)
                extra = ref[s, pl.ds(BLOCK, BIAS_ROWS), :].astype(jnp.float32)
                bias_ref[pl.ds(j, 1), :] = extra[0:1]
        eye = (lax.broadcasted_iota(jnp.int32, (BLOCK, BLOCK), 0)
               == lax.broadcasted_iota(jnp.int32, (BLOCK, BLOCK), 1)).astype(jnp.float32)
        bias_col = lax.dot_general(eye, bias_ref[...], (((1,), (1,)), ((), ())),
                                   preferred_element_type=jnp.float32,
                                   precision=lax.Precision.HIGHEST)
        for j in range(n_cand_blocks):
            tabf_ref[pl.ds(j * BLOCK, BLOCK), pl.ds(BLOCK, 128)] = jnp.broadcast_to(
                bias_col[:, j:j + 1], (BLOCK, 128))
        issue(0, 0)

    slot = b % 2

    @pl.when(b + 1 < n_blocks)
    def _():
        issue(b + 1, 1 - slot)

    q = (qa_ref[...] + qb_ref[...]).astype(jnp.bfloat16)
    qf = q.astype(jnp.float32)
    tcol = tcol_ref[...]
    lane = lax.broadcasted_iota(jnp.int32, (BLOCK, BLOCK), 1)
    length = lens_ref[b]
    n_groups = (length + GROUP - 1) // GROUP

    pltpu.make_async_copy(pos_ref.at[slot], pos_ref.at[slot], sem.at[slot]).wait()
    pos_ext = pos_ref[slot]
    positive = pos_ext[:, 0:BLOCK]
    pos_logit = jnp.sum(qf * positive, axis=1, keepdims=True) - pos_ext[:, BLOCK:BLOCK + 1]

    def pass_a(g, m):
        for i in range(GROUP):
            k = g * GROUP + i
            j = lists_ref[b * list_width + k]
            cand = tabb_ref[j]
            logits = lax.dot_general(q, cand, (((1,), (1,)), ((), ())),
                                     preferred_element_type=jnp.float32) - bias_ref[pl.ds(j, 1), :]
            usable = jnp.logical_and((lane + j * BLOCK) != tcol, k < length)
            masked = jnp.where(usable, logits, NEG_FILL)
            ls_ref[k] = masked
            m = jnp.maximum(m, jnp.max(masked, axis=1, keepdims=True))
        return m

    m = lax.fori_loop(0, n_groups, pass_a, pos_logit)

    def pass_b(g, s):
        for i in range(GROUP):
            s = s + jnp.exp(ls_ref[g * GROUP + i] - m)
        return s

    s_vec = lax.fori_loop(0, n_groups, pass_b, jnp.zeros((BLOCK, BLOCK), jnp.float32))
    row_sum = jnp.exp(pos_logit - m) + jnp.sum(s_vec, axis=1, keepdims=True)
    log_total = m + jnp.log(row_sum)

    acc_ref[...] = jnp.zeros_like(acc_ref)

    def pass_c(g, carry):
        part = None
        for i in range(GROUP):
            k = g * GROUP + i
            j = lists_ref[b * list_width + k]
            w = jnp.exp(ls_ref[k] - log_total).astype(jnp.bfloat16)
            d = jnp.dot(w, tabb_ref[j], preferred_element_type=jnp.float32)
            part = d if part is None else part + d
        acc_ref[...] += part
        return carry

    lax.fori_loop(0, n_groups, pass_c, 0)
    qg = acc_ref[...] + (jnp.exp(pos_logit - log_total) - 1.0) * positive
    qg_ref[...] = qg.astype(qg_ref.dtype)
    loss_ref[...] = log_total - pos_logit


def score(q_mine, q_sent, target_slot, block_lists, list_lens, tab_a, tab_b, parity, dists):
    rows, embed = q_mine.shape
    n_blocks = rows // BLOCK
    n_shards = tab_a.shape[0]
    n_cands = 2 * n_shards * BLOCK
    list_width = block_lists.shape[1]
    grid_spec = pltpu.PrefetchScalarGridSpec(
        num_scalar_prefetch=4,
        grid=(n_blocks,),
        in_specs=[
            pl.BlockSpec((BLOCK, embed), lambda b, *_: (b, 0)),
            pl.BlockSpec((BLOCK, embed), lambda b, *_: (b, 0)),
            pl.BlockSpec((BLOCK, 1), lambda b, *_: (b, 0)),
            pl.BlockSpec(memory_space=pltpu.VMEM),
            pl.BlockSpec(memory_space=pltpu.VMEM),
        ],
        out_specs=[
            pl.BlockSpec((BLOCK, embed), lambda b, *_: (b, 0)),
            pl.BlockSpec((BLOCK, 1), lambda b, *_: (b, 0)),
        ],
        scratch_shapes=[
            pltpu.VMEM((2 * n_shards, BLOCK, embed), jnp.bfloat16),
            pltpu.VMEM((n_cands, EXT), jnp.float32),
            pltpu.VMEM((2 * n_shards, BLOCK), jnp.float32),
            pltpu.VMEM((2, BLOCK, EXT), jnp.float32),
            pltpu.VMEM((list_width, BLOCK, BLOCK), jnp.float32),
            pltpu.VMEM((BLOCK, embed), jnp.float32),
            pltpu.SemaphoreType.DMA((2,)),
        ],
    )
    flops = 2 * 2 * rows * embed * BLOCK * 8
    qg, loss = pl.pallas_call(
        functools.partial(score_kernel, list_width, n_blocks, dists),
        grid_spec=grid_spec,
        out_shape=[
            jax.ShapeDtypeStruct((rows, embed), jnp.bfloat16),
            jax.ShapeDtypeStruct((rows, 1), jnp.float32),
        ],
        compiler_params=pltpu.CompilerParams(
            dimension_semantics=("arbitrary",),
            vmem_limit_bytes=62 * 1024 * 1024,
        ),
        cost_estimate=pl.CostEstimate(
            flops=flops, transcendentals=2 * rows * BLOCK * 8,
            bytes_accessed=2 * tab_a.size * 2 + rows * embed * 4),
    )(block_lists.reshape(-1), list_lens, target_slot, parity,
      q_mine, q_sent, target_slot.reshape(rows, 1), tab_a, tab_b)
    return qg, loss.reshape(rows)


def shards(hidden_rows, w_proj, panels, cand_ids, counts, target_slot, block_lists, list_lens):
    halves, rows_dev, width_half = hidden_rows.shape
    flat_rows = hidden_rows.reshape(halves * rows_dev, width_half)
    n_sec = lax.axis_size("section")
    sec = lax.axis_index("section")
    partner = [(i, i ^ 1) for i in range(n_sec)]
    partial = jnp.dot(flat_rows, w_proj, preferred_element_type=jnp.float32).reshape(halves, rows_dev, -1)
    n_pos = lax.axis_size("pos")
    core = lax.axis_index("pos") % 2
    n_own = lax.axis_size("owner")
    me = sec * n_own + lax.axis_index("owner")
    own_bias = jnp.log(counts[cand_ids].astype(jnp.float32)).astype(jnp.bfloat16)
    own_bias = own_bias.reshape(panels.shape[0] // BLOCK, BLOCK)
    my_block = lax.dynamic_slice_in_dim(panels, core * BLOCK, BLOCK, axis=0)
    my_bias = jnp.pad(lax.dynamic_slice_in_dim(own_bias, core, 1, axis=0), ((0, BIAS_ROWS - 1), (0, 0)))
    buf = jnp.concatenate([my_block, my_bias], axis=0)[None]
    partial, buf = lax.optimization_barrier((partial, buf))
    n_group = n_sec * n_own
    dists = []
    d = n_group // 2
    while d >= 1:
        got = lax.ppermute(buf, ("section", "owner"), [(i, i ^ d) for i in range(n_group)])
        buf = jnp.concatenate([buf, got], axis=0)
        dists.append(d)
        d //= 2
    tab_b = lax.ppermute(buf, "pos", [(i, i ^ 1) for i in range(n_pos)])
    parity = jnp.stack([core, me]).astype(jnp.int32)
    mine = lax.dynamic_index_in_dim(partial, sec, 0, keepdims=False)
    theirs = lax.dynamic_index_in_dim(partial, 1 - sec, 0, keepdims=False)
    n_chunks = 2
    rows_chunk = rows_dev // n_chunks
    blocks_chunk = rows_chunk // BLOCK
    grads, losses, others = [], [], []
    for c in range(n_chunks):
        rows = slice(c * rows_chunk, (c + 1) * rows_chunk)
        blocks = slice(c * blocks_chunk, (c + 1) * blocks_chunk)
        sent = lax.ppermute(theirs[rows], "section", partner)
        grad, loss = score(mine[rows], sent, target_slot[rows], block_lists[blocks], list_lens[blocks], buf, tab_b,
                           parity, tuple(dists))
        grads.append(grad)
        losses.append(loss)
        others.append(lax.ppermute(grad, "section", partner))
    query_grad = jnp.concatenate(grads, axis=0)
    other_grad = jnp.concatenate(others, axis=0)
    position_loss = jnp.concatenate(losses, axis=0)
    both = jnp.where(sec == 0, jnp.concatenate([query_grad, other_grad], axis=0),
                     jnp.concatenate([other_grad, query_grad], axis=0))
    trunk_grad = lax.dot_general(
        both,
        w_proj,
        (((1,), (1,)), ((), ())),
        preferred_element_type=jnp.float32,
    ).astype(jnp.bfloat16)
    return (query_grad, position_loss, trunk_grad.reshape(halves, rows_dev, width_half))


def solution(mesh):
    return jax.shard_map(
        shards,
        mesh=mesh,
        in_specs=(
            P(None, ("owner", "pos"), "section"),
            P("section", None),
            P(("section", "owner"), None),
            P(("section", "owner")),
            P(),
            P(("section", "owner", "pos")),
            P(("section", "owner", "pos"), None),
            P(("section", "owner", "pos")),
        ),
        out_specs=(
            P(("section", "owner", "pos"), None),
            P(("section", "owner", "pos")),
            P(None, ("owner", "pos"), "section"),
        ),
        check_vma=False,
    )
```

```python
import functools

import jax
import jax.numpy as jnp
from jax import lax
from jax.experimental import pallas as pl
from jax.experimental.pallas import tpu as pltpu
from jax.sharding import PartitionSpec as P


BLOCK = 256
NEG_FILL = -1e30
BIAS_ROWS = 16
GROUP = 4
EXT = BLOCK + 128


def score_kernel(list_width, n_blocks, aways,
                 lists_ref, lens_ref, tgt_ref, par_ref,
                 qa_ref, qb_ref, tcol_ref, tab_a_ref, tab_b_ref,
                 qg_ref, loss_ref,
                 tabb_ref, tabf_ref, bias_ref, pos_ref, ls_ref, acc_ref, sem):
    b = pl.program_id(0)
    n_shards = tab_a_ref.shape[0]
    n_cand_blocks = 2 * n_shards

    def issue(block, slot):
        def one(r, carry):
            t = tgt_ref[block * BLOCK + r]
            pltpu.make_async_copy(tabf_ref.at[pl.ds(t, 1), :], pos_ref.at[slot, pl.ds(r, 1), :],
                                  sem.at[slot]).start()
            return carry

        lax.fori_loop(0, BLOCK, one, 0, unroll=8)

    @pl.when(b == 0)
    def _():
        mine = par_ref[0]
        me = par_ref[1]
        for s in range(n_shards):
            away = aways[s]
            for ref, par in ((tab_a_ref, mine), (tab_b_ref, 1 - mine)):
                j = 2 * (me ^ away) + par
                blk = ref[s, pl.ds(0, BLOCK), :]
                tabb_ref[j] = blk
                tabf_ref[pl.ds(pl.multiple_of(j * BLOCK, BLOCK), BLOCK), pl.ds(0, BLOCK)] = blk.astype(jnp.float32)
                extra = ref[s, pl.ds(BLOCK, BIAS_ROWS), :].astype(jnp.float32)
                bias_ref[pl.ds(j, 1), :] = extra[0:1]
        eye = (lax.broadcasted_iota(jnp.int32, (BLOCK, BLOCK), 0)
               == lax.broadcasted_iota(jnp.int32, (BLOCK, BLOCK), 1)).astype(jnp.float32)
        bias_col = lax.dot_general(eye, bias_ref[...], (((1,), (1,)), ((), ())),
                                   preferred_element_type=jnp.float32,
                                   precision=lax.Precision.HIGHEST)
        for j in range(n_cand_blocks):
            tabf_ref[pl.ds(j * BLOCK, BLOCK), pl.ds(BLOCK, 128)] = jnp.broadcast_to(
                bias_col[:, j:j + 1], (BLOCK, 128))
        issue(0, 0)

    slot = b % 2

    @pl.when(b + 1 < n_blocks)
    def _():
        issue(b + 1, 1 - slot)

    q = (qa_ref[...] + qb_ref[...]).astype(jnp.bfloat16)
    qf = q.astype(jnp.float32)
    tcol = tcol_ref[...]
    lane = lax.broadcasted_iota(jnp.int32, (BLOCK, BLOCK), 1)
    length = lens_ref[b]
    n_groups = (length + GROUP - 1) // GROUP

    pltpu.make_async_copy(pos_ref.at[slot], pos_ref.at[slot], sem.at[slot]).wait()
    pos_ext = pos_ref[slot]
    positive = pos_ext[:, 0:BLOCK]
    pos_logit = jnp.sum(qf * positive, axis=1, keepdims=True) - pos_ext[:, BLOCK:BLOCK + 1]

    def pass_a(g, m):
        for i in range(GROUP):
            k = g * GROUP + i
            j = lists_ref[b * list_width + k]
            cand = tabb_ref[j]
            logits = lax.dot_general(q, cand, (((1,), (1,)), ((), ())),
                                     preferred_element_type=jnp.float32) - bias_ref[pl.ds(j, 1), :]
            usable = jnp.logical_and((lane + j * BLOCK) != tcol, k < length)
            masked = jnp.where(usable, logits, NEG_FILL)
            ls_ref[k] = masked
            m = jnp.maximum(m, jnp.max(masked, axis=1, keepdims=True))
        return m

    m = lax.fori_loop(0, n_groups, pass_a, pos_logit)

    def pass_b(g, s):
        for i in range(GROUP):
            s = s + jnp.exp(ls_ref[g * GROUP + i] - m)
        return s

    s_vec = lax.fori_loop(0, n_groups, pass_b, jnp.zeros((BLOCK, BLOCK), jnp.float32))
    row_sum = jnp.exp(pos_logit - m) + jnp.sum(s_vec, axis=1, keepdims=True)
    log_total = m + jnp.log(row_sum)

    acc_ref[...] = jnp.zeros_like(acc_ref)

    def pass_c(g, carry):
        part = None
        for i in range(GROUP):
            k = g * GROUP + i
            j = lists_ref[b * list_width + k]
            w = jnp.exp(ls_ref[k] - log_total).astype(jnp.bfloat16)
            d = jnp.dot(w, tabb_ref[j], preferred_element_type=jnp.float32)
            part = d if part is None else part + d
        acc_ref[...] += part
        return carry

    lax.fori_loop(0, n_groups, pass_c, 0)
    qg = acc_ref[...] + (jnp.exp(pos_logit - log_total) - 1.0) * positive
    qg_ref[...] = qg.astype(qg_ref.dtype)
    loss_ref[...] = log_total - pos_logit


def score(q_mine, q_sent, target_slot, block_lists, list_lens, tab_a, tab_b, parity, aways):
    rows, embed = q_mine.shape
    n_blocks = rows // BLOCK
    n_shards = tab_a.shape[0]
    n_cands = 2 * n_shards * BLOCK
    list_width = block_lists.shape[1]
    grid_spec = pltpu.PrefetchScalarGridSpec(
        num_scalar_prefetch=4,
        grid=(n_blocks,),
        in_specs=[
            pl.BlockSpec((BLOCK, embed), lambda b, *_: (b, 0)),
            pl.BlockSpec((BLOCK, embed), lambda b, *_: (b, 0)),
            pl.BlockSpec((BLOCK, 1), lambda b, *_: (b, 0)),
            pl.BlockSpec(memory_space=pltpu.VMEM),
            pl.BlockSpec(memory_space=pltpu.VMEM),
        ],
        out_specs=[
            pl.BlockSpec((BLOCK, embed), lambda b, *_: (b, 0)),
            pl.BlockSpec((BLOCK, 1), lambda b, *_: (b, 0)),
        ],
        scratch_shapes=[
            pltpu.VMEM((2 * n_shards, BLOCK, embed), jnp.bfloat16),
            pltpu.VMEM((n_cands, EXT), jnp.float32),
            pltpu.VMEM((2 * n_shards, BLOCK), jnp.float32),
            pltpu.VMEM((2, BLOCK, EXT), jnp.float32),
            pltpu.VMEM((list_width, BLOCK, BLOCK), jnp.float32),
            pltpu.VMEM((BLOCK, embed), jnp.float32),
            pltpu.SemaphoreType.DMA((2,)),
        ],
    )
    flops = 2 * 2 * rows * embed * BLOCK * 8
    qg, loss = pl.pallas_call(
        functools.partial(score_kernel, list_width, n_blocks, aways),
        grid_spec=grid_spec,
        out_shape=[
            jax.ShapeDtypeStruct((rows, embed), jnp.bfloat16),
            jax.ShapeDtypeStruct((rows, 1), jnp.float32),
        ],
        compiler_params=pltpu.CompilerParams(
            dimension_semantics=("arbitrary",),
            vmem_limit_bytes=62 * 1024 * 1024,
        ),
        cost_estimate=pl.CostEstimate(
            flops=flops, transcendentals=2 * rows * BLOCK * 8,
            bytes_accessed=2 * tab_a.size * 2 + rows * embed * 4),
    )(block_lists.reshape(-1), list_lens, target_slot, parity,
      q_mine, q_sent, target_slot.reshape(rows, 1), tab_a, tab_b)
    return qg, loss.reshape(rows)


def shards(hidden_rows, w_proj, panels, cand_ids, counts, target_slot, block_lists, list_lens):
    halves, rows_dev, width_half = hidden_rows.shape
    flat_rows = hidden_rows.reshape(halves * rows_dev, width_half)
    n_sec = lax.axis_size("section")
    sec = lax.axis_index("section")
    partner = [(i, i ^ 1) for i in range(n_sec)]
    partial = jnp.dot(flat_rows, w_proj, preferred_element_type=jnp.float32).reshape(halves, rows_dev, -1)
    n_pos = lax.axis_size("pos")
    core = lax.axis_index("pos") % 2
    n_own = lax.axis_size("owner")
    me = sec * n_own + lax.axis_index("owner")
    own_bias = jnp.log(counts[cand_ids].astype(jnp.float32)).astype(jnp.bfloat16)
    own_bias = own_bias.reshape(panels.shape[0] // BLOCK, BLOCK)
    my_block = lax.dynamic_slice_in_dim(panels, core * BLOCK, BLOCK, axis=0)
    my_bias = jnp.pad(lax.dynamic_slice_in_dim(own_bias, core, 1, axis=0), ((0, BIAS_ROWS - 1), (0, 0)))
    buf = jnp.concatenate([my_block, my_bias], axis=0)[None]
    partial, buf = lax.optimization_barrier((partial, buf))
    n_group = n_sec * n_own
    group = ("section", "owner")

    def swap(x, d):
        return lax.ppermute(x, group, [(i, i ^ d) for i in range(n_group)])

    if n_group == 16:
        got = [swap(buf, 4 * m) for m in range(1, 4)]
        buf = jnp.concatenate([buf] + got, axis=0)
        g1, g3 = swap(buf, 1), swap(buf, 3)
        h1, h2 = swap(g3[0:2], 1), swap(g1[2:4], 3)
        buf = jnp.concatenate([buf, g1, g3, h1, h2], axis=0)
        xs = [4 * k for k in range(4)]
        aways = xs + [1 ^ a for a in xs] + [3 ^ a for a in xs] + [2 ^ a for a in xs]
    else:
        aways = [0]
        d = n_group // 2
        while d >= 1:
            buf = jnp.concatenate([buf, swap(buf, d)], axis=0)
            aways = aways + [d ^ a for a in aways]
            d //= 2
    tab_b = lax.ppermute(buf, "pos", [(i, i ^ 1) for i in range(n_pos)])
    parity = jnp.stack([core, me]).astype(jnp.int32)
    mine = lax.dynamic_index_in_dim(partial, sec, 0, keepdims=False)
    theirs = lax.dynamic_index_in_dim(partial, 1 - sec, 0, keepdims=False)
    n_chunks = 2
    rows_chunk = rows_dev // n_chunks
    blocks_chunk = rows_chunk // BLOCK
    grads, losses, others = [], [], []
    for c in range(n_chunks):
        rows = slice(c * rows_chunk, (c + 1) * rows_chunk)
        blocks = slice(c * blocks_chunk, (c + 1) * blocks_chunk)
        sent = lax.ppermute(theirs[rows], "section", partner)
        grad, loss = score(mine[rows], sent, target_slot[rows], block_lists[blocks], list_lens[blocks], buf, tab_b,
                           parity, tuple(aways))
        grads.append(grad)
        losses.append(loss)
        others.append(lax.ppermute(grad, "section", partner))
    query_grad = jnp.concatenate(grads, axis=0)
    other_grad = jnp.concatenate(others, axis=0)
    position_loss = jnp.concatenate(losses, axis=0)
    both = jnp.where(sec == 0, jnp.concatenate([query_grad, other_grad], axis=0),
                     jnp.concatenate([other_grad, query_grad], axis=0))
    trunk_grad = lax.dot_general(
        both,
        w_proj,
        (((1,), (1,)), ((), ())),
        preferred_element_type=jnp.float32,
    ).astype(jnp.bfloat16)
    return (query_grad, position_loss, trunk_grad.reshape(halves, rows_dev, width_half))


def solution(mesh):
    return jax.shard_map(
        shards,
        mesh=mesh,
        in_specs=(
            P(None, ("owner", "pos"), "section"),
            P("section", None),
            P(("section", "owner"), None),
            P(("section", "owner")),
            P(),
            P(("section", "owner", "pos")),
            P(("section", "owner", "pos"), None),
            P(("section", "owner", "pos")),
        ),
        out_specs=(
            P(("section", "owner", "pos"), None),
            P(("section", "owner", "pos")),
            P(None, ("owner", "pos"), "section"),
        ),
        check_vma=False,
    )
```

```python
import functools

import jax
import jax.numpy as jnp
from jax import lax
from jax.experimental import pallas as pl
from jax.experimental.pallas import tpu as pltpu
from jax.sharding import PartitionSpec as P


BLOCK = 256
NEG_FILL = -1e30
BIAS_ROWS = 16
GROUP = 4
EXT = BLOCK + 128


def score_kernel(list_width, n_blocks, aways, n_prev,
                 lists_ref, lens_ref, tgt_ref, par_ref,
                 qa_ref, qb_ref, tcol_ref, tab_a_ref, tab_b_ref, *refs):
    (qg_ref, loss_ref, tabb_ref, tabf_ref, bias_ref, pos_ref, ls_ref, acc_ref, sem) = refs[n_prev:]
    _score_body(list_width, n_blocks, aways, lists_ref, lens_ref, tgt_ref, par_ref,
                qa_ref, qb_ref, tcol_ref, tab_a_ref, tab_b_ref, qg_ref, loss_ref,
                tabb_ref, tabf_ref, bias_ref, pos_ref, ls_ref, acc_ref, sem)


def _score_body(list_width, n_blocks, aways,
                 lists_ref, lens_ref, tgt_ref, par_ref,
                 qa_ref, qb_ref, tcol_ref, tab_a_ref, tab_b_ref,
                 qg_ref, loss_ref,
                 tabb_ref, tabf_ref, bias_ref, pos_ref, ls_ref, acc_ref, sem):
    b = pl.program_id(0)
    n_shards = tab_a_ref.shape[0]
    n_cand_blocks = 2 * n_shards

    def issue(block, slot):
        def one(r, carry):
            t = tgt_ref[block * BLOCK + r]
            pltpu.make_async_copy(tabf_ref.at[pl.ds(t, 1), :], pos_ref.at[slot, pl.ds(r, 1), :],
                                  sem.at[slot]).start()
            return carry

        lax.fori_loop(0, BLOCK, one, 0, unroll=8)

    @pl.when(b == 0)
    def _():
        mine = par_ref[0]
        me = par_ref[1]
        for s in range(n_shards):
            away = aways[s]
            for ref, par in ((tab_a_ref, mine), (tab_b_ref, 1 - mine)):
                j = 2 * (me ^ away) + par
                blk = ref[s, pl.ds(0, BLOCK), :]
                tabb_ref[j] = blk
                tabf_ref[pl.ds(pl.multiple_of(j * BLOCK, BLOCK), BLOCK), pl.ds(0, BLOCK)] = blk.astype(jnp.float32)
                extra = ref[s, pl.ds(BLOCK, BIAS_ROWS), :].astype(jnp.float32)
                bias_ref[pl.ds(j, 1), :] = extra[0:1]
        eye = (lax.broadcasted_iota(jnp.int32, (BLOCK, BLOCK), 0)
               == lax.broadcasted_iota(jnp.int32, (BLOCK, BLOCK), 1)).astype(jnp.float32)
        bias_col = lax.dot_general(eye, bias_ref[...], (((1,), (1,)), ((), ())),
                                   preferred_element_type=jnp.float32,
                                   precision=lax.Precision.HIGHEST)
        for j in range(n_cand_blocks):
            tabf_ref[pl.ds(j * BLOCK, BLOCK), pl.ds(BLOCK, 128)] = jnp.broadcast_to(
                bias_col[:, j:j + 1], (BLOCK, 128))
        issue(0, 0)

    slot = b % 2

    @pl.when(b + 1 < n_blocks)
    def _():
        issue(b + 1, 1 - slot)

    q = (qa_ref[...] + qb_ref[...]).astype(jnp.bfloat16)
    qf = q.astype(jnp.float32)
    tcol = tcol_ref[...]
    lane = lax.broadcasted_iota(jnp.int32, (BLOCK, BLOCK), 1)
    length = lens_ref[b]
    n_groups = (length + GROUP - 1) // GROUP

    pltpu.make_async_copy(pos_ref.at[slot], pos_ref.at[slot], sem.at[slot]).wait()
    pos_ext = pos_ref[slot]
    positive = pos_ext[:, 0:BLOCK]
    pos_logit = jnp.sum(qf * positive, axis=1, keepdims=True) - pos_ext[:, BLOCK:BLOCK + 1]

    def pass_a(g, m):
        for i in range(GROUP):
            k = g * GROUP + i
            j = lists_ref[b * list_width + k]
            cand = tabb_ref[j]
            logits = lax.dot_general(q, cand, (((1,), (1,)), ((), ())),
                                     preferred_element_type=jnp.float32) - bias_ref[pl.ds(j, 1), :]
            usable = jnp.logical_and((lane + j * BLOCK) != tcol, k < length)
            masked = jnp.where(usable, logits, NEG_FILL)
            ls_ref[k] = masked
            m = jnp.maximum(m, jnp.max(masked, axis=1, keepdims=True))
        return m

    m = lax.fori_loop(0, n_groups, pass_a, pos_logit)

    def pass_b(g, s):
        for i in range(GROUP):
            s = s + jnp.exp(ls_ref[g * GROUP + i] - m)
        return s

    s_vec = lax.fori_loop(0, n_groups, pass_b, jnp.zeros((BLOCK, BLOCK), jnp.float32))
    row_sum = jnp.exp(pos_logit - m) + jnp.sum(s_vec, axis=1, keepdims=True)
    log_total = m + jnp.log(row_sum)

    acc_ref[...] = jnp.zeros_like(acc_ref)

    def pass_c(g, carry):
        part = None
        for i in range(GROUP):
            k = g * GROUP + i
            j = lists_ref[b * list_width + k]
            w = jnp.exp(ls_ref[k] - log_total).astype(jnp.bfloat16)
            d = jnp.dot(w, tabb_ref[j], preferred_element_type=jnp.float32)
            part = d if part is None else part + d
        acc_ref[...] += part
        return carry

    lax.fori_loop(0, n_groups, pass_c, 0)
    qg = acc_ref[...] + (jnp.exp(pos_logit - log_total) - 1.0) * positive
    qg_ref[...] = qg.astype(qg_ref.dtype)
    loss_col = jnp.broadcast_to(log_total - pos_logit, (BLOCK, 128))
    loss_ref[...] = jnp.transpose(loss_col)[0:1, :].reshape(loss_ref.shape)


def score(q_mine, q_sent, target_slot, block_lists, list_lens, tab_a, tab_b, parity, aways,
          offset, total_rows, prev=None):
    rows, embed = q_mine.shape
    n_blocks = rows // BLOCK
    first = offset // BLOCK
    n_shards = tab_a.shape[0]
    n_cands = 2 * n_shards * BLOCK
    list_width = block_lists.shape[1]
    prev = () if prev is None else tuple(prev)
    grid_spec = pltpu.PrefetchScalarGridSpec(
        num_scalar_prefetch=4,
        grid=(n_blocks,),
        in_specs=[
            pl.BlockSpec((BLOCK, embed), lambda b, *_: (b, 0)),
            pl.BlockSpec((BLOCK, embed), lambda b, *_: (b, 0)),
            pl.BlockSpec((BLOCK, 1), lambda b, *_: (b, 0)),
            pl.BlockSpec(memory_space=pltpu.VMEM),
            pl.BlockSpec(memory_space=pltpu.VMEM),
        ] + [pl.BlockSpec(memory_space=pl.ANY)] * len(prev),
        out_specs=[
            pl.BlockSpec((BLOCK, embed), lambda b, *_: (b + first, 0)),
            pl.BlockSpec((1, 1, BLOCK), lambda b, *_: (b + first, 0, 0)),
        ],
        scratch_shapes=[
            pltpu.VMEM((2 * n_shards, BLOCK, embed), jnp.bfloat16),
            pltpu.VMEM((n_cands, EXT), jnp.float32),
            pltpu.VMEM((2 * n_shards, BLOCK), jnp.float32),
            pltpu.VMEM((2, BLOCK, EXT), jnp.float32),
            pltpu.VMEM((list_width, BLOCK, BLOCK), jnp.float32),
            pltpu.VMEM((BLOCK, embed), jnp.float32),
            pltpu.SemaphoreType.DMA((2,)),
        ],
    )
    flops = 2 * 2 * rows * embed * BLOCK * 8
    n_in = 4 + 5
    qg, loss = pl.pallas_call(
        functools.partial(score_kernel, list_width, n_blocks, aways, len(prev)),
        grid_spec=grid_spec,
        out_shape=[
            jax.ShapeDtypeStruct((total_rows, embed), jnp.bfloat16),
            jax.ShapeDtypeStruct((total_rows // BLOCK, 1, BLOCK), jnp.float32),
        ],
        input_output_aliases={n_in + i: i for i in range(len(prev))},
        compiler_params=pltpu.CompilerParams(
            dimension_semantics=("arbitrary",),
            vmem_limit_bytes=62 * 1024 * 1024,
        ),
        cost_estimate=pl.CostEstimate(
            flops=flops, transcendentals=2 * rows * BLOCK * 8,
            bytes_accessed=2 * tab_a.size * 2 + rows * embed * 4),
    )(block_lists.reshape(-1), list_lens, target_slot, parity,
      q_mine, q_sent, target_slot.reshape(rows, 1), tab_a, tab_b, *prev)
    return qg, loss


def shards(hidden_rows, w_proj, panels, cand_ids, counts, target_slot, block_lists, list_lens):
    halves, rows_dev, width_half = hidden_rows.shape
    flat_rows = hidden_rows.reshape(halves * rows_dev, width_half)
    n_sec = lax.axis_size("section")
    sec = lax.axis_index("section")
    partner = [(i, i ^ 1) for i in range(n_sec)]
    partial = jnp.dot(flat_rows, w_proj, preferred_element_type=jnp.float32).reshape(halves, rows_dev, -1)
    n_pos = lax.axis_size("pos")
    core = lax.axis_index("pos") % 2
    n_own = lax.axis_size("owner")
    me = sec * n_own + lax.axis_index("owner")
    own_bias = jnp.log(counts[cand_ids].astype(jnp.float32)).astype(jnp.bfloat16)
    own_bias = own_bias.reshape(panels.shape[0] // BLOCK, BLOCK)
    my_block = lax.dynamic_slice_in_dim(panels, core * BLOCK, BLOCK, axis=0)
    my_bias = jnp.pad(lax.dynamic_slice_in_dim(own_bias, core, 1, axis=0), ((0, BIAS_ROWS - 1), (0, 0)))
    buf = jnp.concatenate([my_block, my_bias], axis=0)[None]
    partial, buf = lax.optimization_barrier((partial, buf))
    n_group = n_sec * n_own
    group = ("section", "owner")

    def swap(x, d):
        return lax.ppermute(x, group, [(i, i ^ d) for i in range(n_group)])

    if n_group == 16:
        got = [swap(buf, 4 * m) for m in range(1, 4)]
        buf = jnp.concatenate([buf] + got, axis=0)
        g1, g3 = swap(buf, 1), swap(buf, 3)
        h1, h2 = swap(g3[0:2], 1), swap(g1[2:4], 3)
        buf = jnp.concatenate([buf, g1, g3, h1, h2], axis=0)
        xs = [4 * k for k in range(4)]
        aways = xs + [1 ^ a for a in xs] + [3 ^ a for a in xs] + [2 ^ a for a in xs]
    else:
        aways = [0]
        d = n_group // 2
        while d >= 1:
            buf = jnp.concatenate([buf, swap(buf, d)], axis=0)
            aways = aways + [d ^ a for a in aways]
            d //= 2
    tab_b = lax.ppermute(buf, "pos", [(i, i ^ 1) for i in range(n_pos)])
    parity = jnp.stack([core, me]).astype(jnp.int32)
    mine = lax.dynamic_index_in_dim(partial, sec, 0, keepdims=False)
    theirs = lax.dynamic_index_in_dim(partial, 1 - sec, 0, keepdims=False)
    n_chunks = 2
    rows_chunk = rows_dev // n_chunks
    blocks_chunk = rows_chunk // BLOCK
    outs = None
    others = []
    for c in range(n_chunks):
        rows = slice(c * rows_chunk, (c + 1) * rows_chunk)
        blocks = slice(c * blocks_chunk, (c + 1) * blocks_chunk)
        sent = lax.ppermute(theirs[rows], "section", partner)
        outs = score(mine[rows], sent, target_slot[rows], block_lists[blocks], list_lens[blocks], buf, tab_b,
                     parity, tuple(aways), c * rows_chunk, rows_dev, outs)
        others.append(lax.ppermute(outs[0][rows], "section", partner))
    query_grad, loss_rows = outs
    position_loss = loss_rows.reshape(rows_dev)

    def to_trunk(g):
        return lax.dot_general(g, w_proj, (((1,), (1,)), ((), ())),
                               preferred_element_type=jnp.float32).astype(jnp.bfloat16)

    trunk_grad = jnp.zeros((halves, rows_dev, width_half), jnp.bfloat16)
    trunk_grad = lax.dynamic_update_slice(trunk_grad, to_trunk(query_grad)[None], (sec, 0, 0))
    for c in range(n_chunks):
        trunk_grad = lax.dynamic_update_slice(trunk_grad, to_trunk(others[c])[None], (1 - sec, c * rows_chunk, 0))
    return (query_grad, position_loss, trunk_grad)


def solution(mesh):
    return jax.shard_map(
        shards,
        mesh=mesh,
        in_specs=(
            P(None, ("owner", "pos"), "section"),
            P("section", None),
            P(("section", "owner"), None),
            P(("section", "owner")),
            P(),
            P(("section", "owner", "pos")),
            P(("section", "owner", "pos"), None),
            P(("section", "owner", "pos")),
        ),
        out_specs=(
            P(("section", "owner", "pos"), None),
            P(("section", "owner", "pos")),
            P(None, ("owner", "pos"), "section"),
        ),
        check_vma=False,
    )
```

```python
import functools

import jax
import jax.numpy as jnp
from jax import lax
from jax.experimental import pallas as pl
from jax.experimental.pallas import tpu as pltpu
from jax.sharding import PartitionSpec as P


BLOCK = 256
NEG_FILL = -1e30
BIAS_ROWS = 16
GROUP = 4
EXT = BLOCK + 128


def score_kernel(list_width, n_blocks, aways, n_prev,
                 lists_ref, lens_ref, tgt_ref, par_ref,
                 qa_ref, qb_ref, tcol_ref, tab_a_ref, tab_b_ref, *refs):
    (qg_ref, loss_ref, tabb_ref, tabf_ref, bias_ref, pos_ref, ls_ref, acc_ref, sem) = refs[n_prev:]
    _score_body(list_width, n_blocks, aways, lists_ref, lens_ref, tgt_ref, par_ref,
                qa_ref, qb_ref, tcol_ref, tab_a_ref, tab_b_ref, qg_ref, loss_ref,
                tabb_ref, tabf_ref, bias_ref, pos_ref, ls_ref, acc_ref, sem)


def _score_body(list_width, n_blocks, aways,
                 lists_ref, lens_ref, tgt_ref, par_ref,
                 qa_ref, qb_ref, tcol_ref, tab_a_ref, tab_b_ref,
                 qg_ref, loss_ref,
                 tabb_ref, tabf_ref, bias_ref, pos_ref, ls_ref, acc_ref, sem):
    b = pl.program_id(0)
    n_shards = tab_a_ref.shape[0]
    n_cand_blocks = 2 * n_shards

    def issue(block, slot):
        def one(r, carry):
            t = tgt_ref[block * BLOCK + r]
            pltpu.make_async_copy(tabf_ref.at[pl.ds(t, 1), :], pos_ref.at[slot, pl.ds(r, 1), :],
                                  sem.at[slot]).start()
            return carry

        lax.fori_loop(0, BLOCK, one, 0, unroll=8)

    @pl.when(b == 0)
    def _():
        mine = par_ref[0]
        me = par_ref[1]
        for s in range(n_shards):
            away = aways[s]
            for ref, par in ((tab_a_ref, mine), (tab_b_ref, 1 - mine)):
                j = 2 * (me ^ away) + par
                blk = ref[s, pl.ds(0, BLOCK), :]
                tabb_ref[j] = blk
                tabf_ref[pl.ds(pl.multiple_of(j * BLOCK, BLOCK), BLOCK), pl.ds(0, BLOCK)] = blk.astype(jnp.float32)
                extra = ref[s, pl.ds(BLOCK, BIAS_ROWS), :].astype(jnp.float32)
                bias_ref[pl.ds(j, 1), :] = extra[0:1]
        eye = (lax.broadcasted_iota(jnp.int32, (BLOCK, BLOCK), 0)
               == lax.broadcasted_iota(jnp.int32, (BLOCK, BLOCK), 1)).astype(jnp.float32)
        bias_col = lax.dot_general(eye, bias_ref[...], (((1,), (1,)), ((), ())),
                                   preferred_element_type=jnp.float32,
                                   precision=lax.Precision.HIGHEST)
        for j in range(n_cand_blocks):
            tabf_ref[pl.ds(j * BLOCK, BLOCK), pl.ds(BLOCK, 128)] = jnp.broadcast_to(
                bias_col[:, j:j + 1], (BLOCK, 128))
        issue(0, 0)

    slot = b % 2

    @pl.when(b + 1 < n_blocks)
    def _():
        issue(b + 1, 1 - slot)

    q = (qa_ref[...] + qb_ref[...]).astype(jnp.bfloat16)
    qf = q.astype(jnp.float32)
    tcol = tcol_ref[...]
    lane = lax.broadcasted_iota(jnp.int32, (BLOCK, BLOCK), 1)
    length = lens_ref[b]
    n_groups = (length + GROUP - 1) // GROUP

    pltpu.make_async_copy(pos_ref.at[slot], pos_ref.at[slot], sem.at[slot]).wait()
    pos_ext = pos_ref[slot]
    positive = pos_ext[:, 0:BLOCK]
    pos_logit = jnp.sum(qf * positive, axis=1, keepdims=True) - pos_ext[:, BLOCK:BLOCK + 1]

    def pass_a(g, m):
        for i in range(GROUP):
            k = g * GROUP + i
            j = lists_ref[b * list_width + k]
            cand = tabb_ref[j]
            logits = lax.dot_general(q, cand, (((1,), (1,)), ((), ())),
                                     preferred_element_type=jnp.float32) - bias_ref[pl.ds(j, 1), :]
            usable = jnp.logical_and((lane + j * BLOCK) != tcol, k < length)
            masked = jnp.where(usable, logits, NEG_FILL)
            ls_ref[k] = masked
            m = jnp.maximum(m, jnp.max(masked, axis=1, keepdims=True))
        return m

    m = lax.fori_loop(0, n_groups, pass_a, pos_logit)

    def pass_b(g, s):
        for i in range(GROUP):
            s = s + jnp.exp(ls_ref[g * GROUP + i] - m)
        return s

    s_vec = lax.fori_loop(0, n_groups, pass_b, jnp.zeros((BLOCK, BLOCK), jnp.float32))
    row_sum = jnp.exp(pos_logit - m) + jnp.sum(s_vec, axis=1, keepdims=True)
    log_total = m + jnp.log(row_sum)

    acc_ref[...] = jnp.zeros_like(acc_ref)

    def pass_c(g, carry):
        part = None
        for i in range(GROUP):
            k = g * GROUP + i
            j = lists_ref[b * list_width + k]
            w = jnp.exp(ls_ref[k] - log_total).astype(jnp.bfloat16)
            d = jnp.dot(w, tabb_ref[j], preferred_element_type=jnp.float32)
            part = d if part is None else part + d
        acc_ref[...] += part
        return carry

    lax.fori_loop(0, n_groups, pass_c, 0)
    qg = acc_ref[...] + (jnp.exp(pos_logit - log_total) - 1.0) * positive
    qg_ref[...] = qg.astype(qg_ref.dtype)
    loss_col = jnp.broadcast_to(log_total - pos_logit, (BLOCK, 128))
    loss_ref[...] = jnp.transpose(loss_col)[0:1, :].reshape(loss_ref.shape)


def score(q_mine, q_sent, target_slot, block_lists, list_lens, tab_a, tab_b, parity, aways,
          offset, total_rows, prev=None):
    rows, embed = q_mine.shape
    n_blocks = rows // BLOCK
    first = offset // BLOCK
    n_shards = tab_a.shape[0]
    n_cands = 2 * n_shards * BLOCK
    list_width = block_lists.shape[1]
    prev = () if prev is None else tuple(prev)
    grid_spec = pltpu.PrefetchScalarGridSpec(
        num_scalar_prefetch=4,
        grid=(n_blocks,),
        in_specs=[
            pl.BlockSpec((BLOCK, embed), lambda b, *_: (b, 0)),
            pl.BlockSpec((BLOCK, embed), lambda b, *_: (b, 0)),
            pl.BlockSpec((BLOCK, 1), lambda b, *_: (b, 0)),
            pl.BlockSpec(memory_space=pltpu.VMEM),
            pl.BlockSpec(memory_space=pltpu.VMEM),
        ] + [pl.BlockSpec(memory_space=pl.ANY)] * len(prev),
        out_specs=[
            pl.BlockSpec((BLOCK, embed), lambda b, *_: (b + first, 0)),
            pl.BlockSpec((1, 1, BLOCK), lambda b, *_: (b + first, 0, 0)),
        ],
        scratch_shapes=[
            pltpu.VMEM((2 * n_shards, BLOCK, embed), jnp.bfloat16),
            pltpu.VMEM((n_cands, EXT), jnp.float32),
            pltpu.VMEM((2 * n_shards, BLOCK), jnp.float32),
            pltpu.VMEM((2, BLOCK, EXT), jnp.float32),
            pltpu.VMEM((list_width, BLOCK, BLOCK), jnp.float32),
            pltpu.VMEM((BLOCK, embed), jnp.float32),
            pltpu.SemaphoreType.DMA((2,)),
        ],
    )
    flops = 2 * 2 * rows * embed * BLOCK * 8
    n_in = 4 + 5
    qg, loss = pl.pallas_call(
        functools.partial(score_kernel, list_width, n_blocks, aways, len(prev)),
        grid_spec=grid_spec,
        out_shape=[
            jax.ShapeDtypeStruct((total_rows, embed), jnp.bfloat16),
            jax.ShapeDtypeStruct((total_rows // BLOCK, 1, BLOCK), jnp.float32),
        ],
        input_output_aliases={n_in + i: i for i in range(len(prev))},
        compiler_params=pltpu.CompilerParams(
            dimension_semantics=("arbitrary",),
            vmem_limit_bytes=62 * 1024 * 1024,
        ),
        cost_estimate=pl.CostEstimate(
            flops=flops, transcendentals=2 * rows * BLOCK * 8,
            bytes_accessed=2 * tab_a.size * 2 + rows * embed * 4),
    )(block_lists.reshape(-1), list_lens, target_slot, parity,
      q_mine, q_sent, target_slot.reshape(rows, 1), tab_a, tab_b, *prev)
    return qg, loss


def shards(hidden_rows, w_proj, panels, cand_ids, counts, target_slot, block_lists, list_lens):
    halves, rows_dev, width_half = hidden_rows.shape
    n_sec = lax.axis_size("section")
    sec = lax.axis_index("section")
    partner = [(i, i ^ 1) for i in range(n_sec)]
    n_pos = lax.axis_size("pos")
    core = lax.axis_index("pos") % 2
    n_own = lax.axis_size("owner")
    me = sec * n_own + lax.axis_index("owner")
    own_bias = jnp.log(counts[cand_ids].astype(jnp.float32)).astype(jnp.bfloat16)
    own_bias = own_bias.reshape(panels.shape[0] // BLOCK, BLOCK)
    my_block = lax.dynamic_slice_in_dim(panels, core * BLOCK, BLOCK, axis=0)
    my_bias = jnp.pad(lax.dynamic_slice_in_dim(own_bias, core, 1, axis=0), ((0, BIAS_ROWS - 1), (0, 0)))
    buf = jnp.concatenate([my_block, my_bias], axis=0)[None]
    n_group = n_sec * n_own
    group = ("section", "owner")

    def swap(x, d):
        return lax.ppermute(x, group, [(i, i ^ d) for i in range(n_group)])

    if n_group == 16:
        got = [swap(buf, 4 * m) for m in range(1, 4)]
        buf = jnp.concatenate([buf] + got, axis=0)
        g1, g3 = swap(buf, 1), swap(buf, 3)
        h1, h2 = swap(g3[0:2], 1), swap(g1[2:4], 3)
        buf = jnp.concatenate([buf, g1, g3, h1, h2], axis=0)
        xs = [4 * k for k in range(4)]
        aways = xs + [1 ^ a for a in xs] + [3 ^ a for a in xs] + [2 ^ a for a in xs]
    else:
        aways = [0]
        d = n_group // 2
        while d >= 1:
            buf = jnp.concatenate([buf, swap(buf, d)], axis=0)
            aways = aways + [d ^ a for a in aways]
            d //= 2
    tab_b = lax.ppermute(buf, "pos", [(i, i ^ 1) for i in range(n_pos)])
    parity = jnp.stack([core, me]).astype(jnp.int32)
    mine_rows = lax.dynamic_index_in_dim(hidden_rows, sec, 0, keepdims=False)
    their_rows = lax.dynamic_index_in_dim(hidden_rows, 1 - sec, 0, keepdims=False)

    def project(x):
        return jnp.dot(x, w_proj, preferred_element_type=jnp.float32)

    n_pblocks = rows_dev // BLOCK
    first_blocks = (n_pblocks * 5 + 7) // 8
    bounds = [0, first_blocks * BLOCK, rows_dev] if 0 < first_blocks < n_pblocks else [0, rows_dev // 2, rows_dev]
    n_chunks = 2
    outs = None
    others = []
    for c in range(n_chunks):
        rows = slice(bounds[c], bounds[c + 1])
        blocks = slice(bounds[c] // BLOCK, bounds[c + 1] // BLOCK)
        sent = lax.ppermute(project(their_rows[rows]), "section", partner)
        outs = score(project(mine_rows[rows]), sent, target_slot[rows], block_lists[blocks], list_lens[blocks],
                     buf, tab_b, parity, tuple(aways), bounds[c], rows_dev, outs)
        others.append(lax.ppermute(outs[0][rows], "section", partner))
    query_grad, loss_rows = outs
    position_loss = loss_rows.reshape(rows_dev)

    def to_trunk(g):
        return lax.dot_general(g, w_proj, (((1,), (1,)), ((), ())),
                               preferred_element_type=jnp.float32).astype(jnp.bfloat16)

    trunk_grad = jnp.zeros((halves, rows_dev, width_half), jnp.bfloat16)
    trunk_grad = lax.dynamic_update_slice(trunk_grad, to_trunk(query_grad)[None], (sec, 0, 0))
    for c in range(n_chunks):
        trunk_grad = lax.dynamic_update_slice(trunk_grad, to_trunk(others[c])[None], (1 - sec, bounds[c], 0))
    return (query_grad, position_loss, trunk_grad)


def solution(mesh):
    return jax.shard_map(
        shards,
        mesh=mesh,
        in_specs=(
            P(None, ("owner", "pos"), "section"),
            P("section", None),
            P(("section", "owner"), None),
            P(("section", "owner")),
            P(),
            P(("section", "owner", "pos")),
            P(("section", "owner", "pos"), None),
            P(("section", "owner", "pos")),
        ),
        out_specs=(
            P(("section", "owner", "pos"), None),
            P(("section", "owner", "pos")),
            P(None, ("owner", "pos"), "section"),
        ),
        check_vma=False,
    )
```

```python
import functools

import jax
import jax.numpy as jnp
from jax import lax
from jax.experimental import pallas as pl
from jax.experimental.pallas import tpu as pltpu
from jax.sharding import PartitionSpec as P


BLOCK = 256
NEG_FILL = -1e30
BIAS_ROWS = 16
GROUP = 4
EXT = BLOCK + 128


def score_kernel(list_width, n_blocks, aways, n_prev,
                 lists_ref, lens_ref, tgt_ref, par_ref,
                 qa_ref, qb_ref, tcol_ref, tab_a_ref, tab_b_ref, *refs):
    (qg_ref, loss_ref, tabb_ref, tabf_ref, bias_ref, pos_ref, ls_ref, acc_ref, sem) = refs[n_prev:]
    _score_body(list_width, n_blocks, aways, lists_ref, lens_ref, tgt_ref, par_ref,
                qa_ref, qb_ref, tcol_ref, tab_a_ref, tab_b_ref, qg_ref, loss_ref,
                tabb_ref, tabf_ref, bias_ref, pos_ref, ls_ref, acc_ref, sem)


def _score_body(list_width, n_blocks, aways,
                 lists_ref, lens_ref, tgt_ref, par_ref,
                 qa_ref, qb_ref, tcol_ref, tab_a_ref, tab_b_ref,
                 qg_ref, loss_ref,
                 tabb_ref, tabf_ref, bias_ref, pos_ref, ls_ref, acc_ref, sem):
    b = pl.program_id(0)
    n_shards = tab_a_ref.shape[0]
    n_cand_blocks = 2 * n_shards

    def issue(block, slot):
        def one(r, carry):
            t = tgt_ref[block * BLOCK + r]
            pltpu.make_async_copy(tabf_ref.at[pl.ds(t, 1), :], pos_ref.at[slot, pl.ds(r, 1), :],
                                  sem.at[slot]).start()
            return carry

        lax.fori_loop(0, BLOCK, one, 0, unroll=8)

    @pl.when(b == 0)
    def _():
        mine = par_ref[0]
        me = par_ref[1]
        for s in range(n_shards):
            away = aways[s]
            for ref, par in ((tab_a_ref, mine), (tab_b_ref, 1 - mine)):
                j = 2 * (me ^ away) + par
                blk = ref[s, pl.ds(0, BLOCK), :]
                tabb_ref[j] = blk
                tabf_ref[pl.ds(pl.multiple_of(j * BLOCK, BLOCK), BLOCK), pl.ds(0, BLOCK)] = blk.astype(jnp.float32)
                extra = ref[s, pl.ds(BLOCK, BIAS_ROWS), :].astype(jnp.float32)
                bias_ref[pl.ds(j, 1), :] = extra[0:1]
        eye = (lax.broadcasted_iota(jnp.int32, (BLOCK, BLOCK), 0)
               == lax.broadcasted_iota(jnp.int32, (BLOCK, BLOCK), 1)).astype(jnp.float32)
        bias_col = lax.dot_general(eye, bias_ref[...], (((1,), (1,)), ((), ())),
                                   preferred_element_type=jnp.float32,
                                   precision=lax.Precision.HIGHEST)
        for j in range(n_cand_blocks):
            tabf_ref[pl.ds(j * BLOCK, BLOCK), pl.ds(BLOCK, 128)] = jnp.broadcast_to(
                bias_col[:, j:j + 1], (BLOCK, 128))
        issue(0, 0)

    slot = b % 2

    @pl.when(b + 1 < n_blocks)
    def _():
        issue(b + 1, 1 - slot)

    q = (qa_ref[...] + qb_ref[...]).astype(jnp.bfloat16)
    qf = q.astype(jnp.float32)
    tcol = tcol_ref[...]
    lane = lax.broadcasted_iota(jnp.int32, (BLOCK, BLOCK), 1)
    length = lens_ref[b]
    n_groups = (length + GROUP - 1) // GROUP

    pltpu.make_async_copy(pos_ref.at[slot], pos_ref.at[slot], sem.at[slot]).wait()
    pos_ext = pos_ref[slot]
    positive = pos_ext[:, 0:BLOCK]
    pos_logit = jnp.sum(qf * positive, axis=1, keepdims=True) - pos_ext[:, BLOCK:BLOCK + 1]

    def pass_a(g, m):
        for i in range(GROUP):
            k = g * GROUP + i
            j = lists_ref[b * list_width + k]
            cand = tabb_ref[j]
            logits = lax.dot_general(q, cand, (((1,), (1,)), ((), ())),
                                     preferred_element_type=jnp.float32) - bias_ref[pl.ds(j, 1), :]
            usable = jnp.logical_and((lane + j * BLOCK) != tcol, k < length)
            masked = jnp.where(usable, logits, NEG_FILL)
            ls_ref[k] = masked
            m = jnp.maximum(m, jnp.max(masked, axis=1, keepdims=True))
        return m

    m = lax.fori_loop(0, n_groups, pass_a, pos_logit)

    def pass_b(g, s):
        for i in range(GROUP):
            s = s + jnp.exp(ls_ref[g * GROUP + i] - m)
        return s

    s_vec = lax.fori_loop(0, n_groups, pass_b, jnp.zeros((BLOCK, BLOCK), jnp.float32))
    row_sum = jnp.exp(pos_logit - m) + jnp.sum(s_vec, axis=1, keepdims=True)
    log_total = m + jnp.log(row_sum)

    acc_ref[...] = jnp.zeros_like(acc_ref)

    def pass_c(g, carry):
        part = None
        for i in range(GROUP):
            k = g * GROUP + i
            j = lists_ref[b * list_width + k]
            w = jnp.exp(ls_ref[k] - log_total).astype(jnp.bfloat16)
            d = jnp.dot(w, tabb_ref[j], preferred_element_type=jnp.float32)
            part = d if part is None else part + d
        acc_ref[...] += part
        return carry

    lax.fori_loop(0, n_groups, pass_c, 0)
    qg = acc_ref[...] + (jnp.exp(pos_logit - log_total) - 1.0) * positive
    qg_ref[...] = qg.astype(qg_ref.dtype)
    loss_col = jnp.broadcast_to(log_total - pos_logit, (BLOCK, 128))
    loss_ref[...] = jnp.transpose(loss_col)[0:1, :].reshape(loss_ref.shape)


def score(q_mine, q_sent, target_slot, block_lists, list_lens, tab_a, tab_b, parity, aways,
          offset, total_rows, prev=None):
    rows, embed = q_mine.shape
    n_blocks = rows // BLOCK
    first = offset // BLOCK
    n_shards = tab_a.shape[0]
    n_cands = 2 * n_shards * BLOCK
    list_width = block_lists.shape[1]
    prev = () if prev is None else tuple(prev)
    grid_spec = pltpu.PrefetchScalarGridSpec(
        num_scalar_prefetch=4,
        grid=(n_blocks,),
        in_specs=[
            pl.BlockSpec((BLOCK, embed), lambda b, *_: (b, 0)),
            pl.BlockSpec((BLOCK, embed), lambda b, *_: (b, 0)),
            pl.BlockSpec((BLOCK, 1), lambda b, *_: (b, 0)),
            pl.BlockSpec(memory_space=pltpu.VMEM),
            pl.BlockSpec(memory_space=pltpu.VMEM),
        ] + [pl.BlockSpec(memory_space=pl.ANY)] * len(prev),
        out_specs=[
            pl.BlockSpec((BLOCK, embed), lambda b, *_: (b + first, 0)),
            pl.BlockSpec((1, 1, BLOCK), lambda b, *_: (b + first, 0, 0)),
        ],
        scratch_shapes=[
            pltpu.VMEM((2 * n_shards, BLOCK, embed), jnp.bfloat16),
            pltpu.VMEM((n_cands, EXT), jnp.float32),
            pltpu.VMEM((2 * n_shards, BLOCK), jnp.float32),
            pltpu.VMEM((2, BLOCK, EXT), jnp.float32),
            pltpu.VMEM((list_width, BLOCK, BLOCK), jnp.float32),
            pltpu.VMEM((BLOCK, embed), jnp.float32),
            pltpu.SemaphoreType.DMA((2,)),
        ],
    )
    flops = 2 * 2 * rows * embed * BLOCK * 8
    n_in = 4 + 5
    qg, loss = pl.pallas_call(
        functools.partial(score_kernel, list_width, n_blocks, aways, len(prev)),
        grid_spec=grid_spec,
        out_shape=[
            jax.ShapeDtypeStruct((total_rows, embed), jnp.bfloat16),
            jax.ShapeDtypeStruct((total_rows // BLOCK, 1, BLOCK), jnp.float32),
        ],
        input_output_aliases={n_in + i: i for i in range(len(prev))},
        compiler_params=pltpu.CompilerParams(
            dimension_semantics=("arbitrary",),
            vmem_limit_bytes=62 * 1024 * 1024,
        ),
        cost_estimate=pl.CostEstimate(
            flops=flops, transcendentals=2 * rows * BLOCK * 8,
            bytes_accessed=2 * tab_a.size * 2 + rows * embed * 4),
    )(block_lists.reshape(-1), list_lens, target_slot, parity,
      q_mine, q_sent, target_slot.reshape(rows, 1), tab_a, tab_b, *prev)
    return qg, loss


def shards(hidden_rows, w_proj, panels, cand_ids, counts, target_slot, block_lists, list_lens):
    halves, rows_dev, width_half = hidden_rows.shape
    n_sec = lax.axis_size("section")
    sec = lax.axis_index("section")
    partner = [(i, i ^ 1) for i in range(n_sec)]
    n_pos = lax.axis_size("pos")
    core = lax.axis_index("pos") % 2
    n_own = lax.axis_size("owner")
    me = sec * n_own + lax.axis_index("owner")
    own_bias = jnp.log(counts[cand_ids].astype(jnp.float32)).astype(jnp.bfloat16)
    own_bias = own_bias.reshape(panels.shape[0] // BLOCK, BLOCK)
    my_block = lax.dynamic_slice_in_dim(panels, core * BLOCK, BLOCK, axis=0)
    my_bias = jnp.pad(lax.dynamic_slice_in_dim(own_bias, core, 1, axis=0), ((0, BIAS_ROWS - 1), (0, 0)))
    buf = jnp.concatenate([my_block, my_bias], axis=0)[None]
    n_group = n_sec * n_own
    group = ("section", "owner")

    def swap(x, d):
        return lax.ppermute(x, group, [(i, i ^ d) for i in range(n_group)])

    if n_group == 16:
        got = [swap(buf, 4 * m) for m in range(1, 4)]
        buf = jnp.concatenate([buf] + got, axis=0)
        g1, g3 = swap(buf, 1), swap(buf, 3)
        h1, h2 = swap(g3[0:2], 1), swap(g1[2:4], 3)
        buf = jnp.concatenate([buf, g1, g3, h1, h2], axis=0)
        xs = [4 * k for k in range(4)]
        aways = xs + [1 ^ a for a in xs] + [3 ^ a for a in xs] + [2 ^ a for a in xs]
    else:
        aways = [0]
        d = n_group // 2
        while d >= 1:
            buf = jnp.concatenate([buf, swap(buf, d)], axis=0)
            aways = aways + [d ^ a for a in aways]
            d //= 2
    tab_b = lax.ppermute(buf, "pos", [(i, i ^ 1) for i in range(n_pos)])
    parity = jnp.stack([core, me]).astype(jnp.int32)
    mine_rows = lax.dynamic_index_in_dim(hidden_rows, sec, 0, keepdims=False)
    their_rows = lax.dynamic_index_in_dim(hidden_rows, 1 - sec, 0, keepdims=False)

    def project(x):
        return jnp.dot(x, w_proj, preferred_element_type=jnp.float32)

    n_pblocks = rows_dev // BLOCK
    first_blocks = (n_pblocks * 5 + 7) // 8
    bounds = [0, first_blocks * BLOCK, rows_dev] if 0 < first_blocks < n_pblocks else [0, rows_dev // 2, rows_dev]
    n_chunks = 2
    outs = None
    others = []
    for c in range(n_chunks):
        rows = slice(bounds[c], bounds[c + 1])
        blocks = slice(bounds[c] // BLOCK, bounds[c + 1] // BLOCK)
        theirs = project(their_rows[rows])
        mine = project(mine_rows[rows])
        sent = lax.ppermute(theirs, "section", partner)
        outs = score(mine, sent, target_slot[rows], block_lists[blocks], list_lens[blocks],
                     buf, tab_b, parity, tuple(aways), bounds[c], rows_dev, outs)
        others.append(lax.ppermute(outs[0][rows], "section", partner))
    query_grad, loss_rows = outs
    position_loss = loss_rows.reshape(rows_dev)

    def to_trunk(g):
        return lax.dot_general(g, w_proj, (((1,), (1,)), ((), ())),
                               preferred_element_type=jnp.float32).astype(jnp.bfloat16)

    trunk_grad = jnp.zeros((halves, rows_dev, width_half), jnp.bfloat16)
    trunk_grad = lax.dynamic_update_slice(trunk_grad, to_trunk(query_grad)[None], (sec, 0, 0))
    for c in range(n_chunks):
        trunk_grad = lax.dynamic_update_slice(trunk_grad, to_trunk(others[c])[None], (1 - sec, bounds[c], 0))
    return (query_grad, position_loss, trunk_grad)


def solution(mesh):
    return jax.shard_map(
        shards,
        mesh=mesh,
        in_specs=(
            P(None, ("owner", "pos"), "section"),
            P("section", None),
            P(("section", "owner"), None),
            P(("section", "owner")),
            P(),
            P(("section", "owner", "pos")),
            P(("section", "owner", "pos"), None),
            P(("section", "owner", "pos")),
        ),
        out_specs=(
            P(("section", "owner", "pos"), None),
            P(("section", "owner", "pos")),
            P(None, ("owner", "pos"), "section"),
        ),
        check_vma=False,
    )
```

```python
import functools

import jax
import jax.numpy as jnp
from jax import lax
from jax.experimental import pallas as pl
from jax.experimental.pallas import tpu as pltpu
from jax.sharding import PartitionSpec as P


BLOCK = 256
NEG_FILL = -1e30
BIAS_ROWS = 16
GROUP = 4
EXT = BLOCK + 128


def score_kernel(list_width, n_blocks, aways, n_prev, first,
                 lists_ref, lens_ref, tgt_ref, par_ref,
                 qa_ref, qb_ref, tcol_ref, tab_a_ref, tab_b_ref, *refs):
    (qg_ref, loss_ref, qgc_ref, tabb_ref, tabf_ref, bias_ref, pos_ref, ls_ref, acc_ref, sem) = refs[n_prev:]
    _score_body(list_width, n_blocks, aways, first, lists_ref, lens_ref, tgt_ref, par_ref,
                qa_ref, qb_ref, tcol_ref, tab_a_ref, tab_b_ref, qg_ref, loss_ref, qgc_ref,
                tabb_ref, tabf_ref, bias_ref, pos_ref, ls_ref, acc_ref, sem)


def _score_body(list_width, n_blocks, aways, first,
                 lists_ref, lens_ref, tgt_ref, par_ref,
                 qa_ref, qb_ref, tcol_ref, tab_a_ref, tab_b_ref,
                 qg_ref, loss_ref, qgc_ref,
                 tabb_ref, tabf_ref, bias_ref, pos_ref, ls_ref, acc_ref, sem):
    b = pl.program_id(0)
    bg = b + first
    n_shards = tab_a_ref.shape[0]
    n_cand_blocks = 2 * n_shards

    def issue(block, slot):
        def one(r, carry):
            t = tgt_ref[(first + block) * BLOCK + r]
            pltpu.make_async_copy(tabf_ref.at[pl.ds(t, 1), :], pos_ref.at[slot, pl.ds(r, 1), :],
                                  sem.at[slot]).start()
            return carry

        lax.fori_loop(0, BLOCK, one, 0, unroll=8)

    @pl.when(b == 0)
    def _():
        mine = par_ref[0]
        me = par_ref[1]
        for s in range(n_shards):
            away = aways[s]
            for ref, par in ((tab_a_ref, mine), (tab_b_ref, 1 - mine)):
                j = 2 * (me ^ away) + par
                blk = ref[s, pl.ds(0, BLOCK), :]
                tabb_ref[j] = blk
                tabf_ref[pl.ds(pl.multiple_of(j * BLOCK, BLOCK), BLOCK), pl.ds(0, BLOCK)] = blk.astype(jnp.float32)
                extra = ref[s, pl.ds(BLOCK, BIAS_ROWS), :].astype(jnp.float32)
                bias_ref[pl.ds(j, 1), :] = extra[0:1]
        eye = (lax.broadcasted_iota(jnp.int32, (BLOCK, BLOCK), 0)
               == lax.broadcasted_iota(jnp.int32, (BLOCK, BLOCK), 1)).astype(jnp.float32)
        bias_col = lax.dot_general(eye, bias_ref[...], (((1,), (1,)), ((), ())),
                                   preferred_element_type=jnp.float32,
                                   precision=lax.Precision.HIGHEST)
        for j in range(n_cand_blocks):
            tabf_ref[pl.ds(j * BLOCK, BLOCK), pl.ds(BLOCK, 128)] = jnp.broadcast_to(
                bias_col[:, j:j + 1], (BLOCK, 128))
        issue(0, 0)

    slot = b % 2

    @pl.when(b + 1 < n_blocks)
    def _():
        issue(b + 1, 1 - slot)

    q = (qa_ref[...] + qb_ref[...]).astype(jnp.bfloat16)
    qf = q.astype(jnp.float32)
    tcol = tcol_ref[...]
    lane = lax.broadcasted_iota(jnp.int32, (BLOCK, BLOCK), 1)
    length = lens_ref[bg]
    n_groups = (length + GROUP - 1) // GROUP

    pltpu.make_async_copy(pos_ref.at[slot], pos_ref.at[slot], sem.at[slot]).wait()
    pos_ext = pos_ref[slot]
    positive = pos_ext[:, 0:BLOCK]
    pos_logit = jnp.sum(qf * positive, axis=1, keepdims=True) - pos_ext[:, BLOCK:BLOCK + 1]

    def pass_a(g, m):
        for i in range(GROUP):
            k = g * GROUP + i
            j = lists_ref[bg * list_width + k]
            cand = tabb_ref[j]
            logits = lax.dot_general(q, cand, (((1,), (1,)), ((), ())),
                                     preferred_element_type=jnp.float32) - bias_ref[pl.ds(j, 1), :]
            usable = jnp.logical_and((lane + j * BLOCK) != tcol, k < length)
            masked = jnp.where(usable, logits, NEG_FILL)
            ls_ref[k] = masked
            m = jnp.maximum(m, jnp.max(masked, axis=1, keepdims=True))
        return m

    m = lax.fori_loop(0, n_groups, pass_a, pos_logit)

    def pass_b(g, s):
        for i in range(GROUP):
            s = s + jnp.exp(ls_ref[g * GROUP + i] - m)
        return s

    s_vec = lax.fori_loop(0, n_groups, pass_b, jnp.zeros((BLOCK, BLOCK), jnp.float32))
    row_sum = jnp.exp(pos_logit - m) + jnp.sum(s_vec, axis=1, keepdims=True)
    log_total = m + jnp.log(row_sum)

    acc_ref[...] = jnp.zeros_like(acc_ref)

    def pass_c(g, carry):
        part = None
        for i in range(GROUP):
            k = g * GROUP + i
            j = lists_ref[bg * list_width + k]
            w = jnp.exp(ls_ref[k] - log_total).astype(jnp.bfloat16)
            d = jnp.dot(w, tabb_ref[j], preferred_element_type=jnp.float32)
            part = d if part is None else part + d
        acc_ref[...] += part
        return carry

    lax.fori_loop(0, n_groups, pass_c, 0)
    qg = acc_ref[...] + (jnp.exp(pos_logit - log_total) - 1.0) * positive
    qg_ref[...] = qg.astype(qg_ref.dtype)
    qgc_ref[...] = qg.astype(qgc_ref.dtype)
    loss_col = jnp.broadcast_to(log_total - pos_logit, (BLOCK, 128))
    loss_ref[...] = jnp.transpose(loss_col)[0:1, :].reshape(loss_ref.shape)


def score(q_mine, q_sent, target_slot, block_lists, list_lens, tab_a, tab_b, parity, aways,
          offset, total_rows, prev=None):
    rows, embed = q_mine.shape
    n_blocks = rows // BLOCK
    first = offset // BLOCK
    n_shards = tab_a.shape[0]
    n_cands = 2 * n_shards * BLOCK
    list_width = block_lists.shape[1]
    prev = () if prev is None else tuple(prev)
    grid_spec = pltpu.PrefetchScalarGridSpec(
        num_scalar_prefetch=4,
        grid=(n_blocks,),
        in_specs=[
            pl.BlockSpec((BLOCK, embed), lambda b, *_: (b, 0)),
            pl.BlockSpec((BLOCK, embed), lambda b, *_: (b, 0)),
            pl.BlockSpec((BLOCK, 1), lambda b, *_: (b + first, 0)),
            pl.BlockSpec(memory_space=pltpu.VMEM),
            pl.BlockSpec(memory_space=pltpu.VMEM),
        ] + [pl.BlockSpec(memory_space=pl.ANY)] * len(prev),
        out_specs=[
            pl.BlockSpec((BLOCK, embed), lambda b, *_: (b + first, 0)),
            pl.BlockSpec((1, 1, BLOCK), lambda b, *_: (b + first, 0, 0)),
            pl.BlockSpec((BLOCK, embed), lambda b, *_: (b, 0)),
        ],
        scratch_shapes=[
            pltpu.VMEM((2 * n_shards, BLOCK, embed), jnp.bfloat16),
            pltpu.VMEM((n_cands, EXT), jnp.float32),
            pltpu.VMEM((2 * n_shards, BLOCK), jnp.float32),
            pltpu.VMEM((2, BLOCK, EXT), jnp.float32),
            pltpu.VMEM((list_width, BLOCK, BLOCK), jnp.float32),
            pltpu.VMEM((BLOCK, embed), jnp.float32),
            pltpu.SemaphoreType.DMA((2,)),
        ],
    )
    flops = 2 * 2 * rows * embed * BLOCK * 8
    n_in = 4 + 5
    qg, loss, qg_chunk = pl.pallas_call(
        functools.partial(score_kernel, list_width, n_blocks, aways, len(prev), first),
        grid_spec=grid_spec,
        out_shape=[
            jax.ShapeDtypeStruct((total_rows, embed), jnp.bfloat16),
            jax.ShapeDtypeStruct((total_rows // BLOCK, 1, BLOCK), jnp.float32),
            jax.ShapeDtypeStruct((rows, embed), jnp.bfloat16),
        ],
        input_output_aliases={n_in + i: i for i in range(len(prev))},
        compiler_params=pltpu.CompilerParams(
            dimension_semantics=("arbitrary",),
            vmem_limit_bytes=62 * 1024 * 1024,
        ),
        cost_estimate=pl.CostEstimate(
            flops=flops, transcendentals=2 * rows * BLOCK * 8,
            bytes_accessed=2 * tab_a.size * 2 + rows * embed * 4),
    )(block_lists.reshape(-1), list_lens, target_slot, parity,
      q_mine, q_sent, target_slot.reshape(total_rows, 1), tab_a, tab_b, *prev)
    return (qg, loss), qg_chunk


def shards(hidden_rows, w_proj, panels, cand_ids, counts, target_slot, block_lists, list_lens):
    halves, rows_dev, width_half = hidden_rows.shape
    n_sec = lax.axis_size("section")
    sec = lax.axis_index("section")
    partner = [(i, i ^ 1) for i in range(n_sec)]
    n_pos = lax.axis_size("pos")
    core = lax.axis_index("pos") % 2
    n_own = lax.axis_size("owner")
    me = sec * n_own + lax.axis_index("owner")
    own_bias = jnp.log(counts[cand_ids].astype(jnp.float32)).astype(jnp.bfloat16)
    own_bias = own_bias.reshape(panels.shape[0] // BLOCK, BLOCK)
    my_block = lax.dynamic_slice_in_dim(panels, core * BLOCK, BLOCK, axis=0)
    my_bias = jnp.pad(lax.dynamic_slice_in_dim(own_bias, core, 1, axis=0), ((0, BIAS_ROWS - 1), (0, 0)))
    buf = jnp.concatenate([my_block, my_bias], axis=0)[None]
    n_group = n_sec * n_own
    group = ("section", "owner")

    def swap(x, d):
        return lax.ppermute(x, group, [(i, i ^ d) for i in range(n_group)])

    if n_group == 16:
        got = [swap(buf, 4 * m) for m in range(1, 4)]
        buf = jnp.concatenate([buf] + got, axis=0)
        g1, g3 = swap(buf, 1), swap(buf, 3)
        h1, h2 = swap(g3[0:2], 1), swap(g1[2:4], 3)
        buf = jnp.concatenate([buf, g1, g3, h1, h2], axis=0)
        xs = [4 * k for k in range(4)]
        aways = xs + [1 ^ a for a in xs] + [3 ^ a for a in xs] + [2 ^ a for a in xs]
    else:
        aways = [0]
        d = n_group // 2
        while d >= 1:
            buf = jnp.concatenate([buf, swap(buf, d)], axis=0)
            aways = aways + [d ^ a for a in aways]
            d //= 2
    tab_b = lax.ppermute(buf, "pos", [(i, i ^ 1) for i in range(n_pos)])
    parity = jnp.stack([core, me]).astype(jnp.int32)
    mine_rows = lax.dynamic_index_in_dim(hidden_rows, sec, 0, keepdims=False)
    their_rows = lax.dynamic_index_in_dim(hidden_rows, 1 - sec, 0, keepdims=False)

    def project(x):
        return jnp.dot(x, w_proj, preferred_element_type=jnp.float32)

    n_pblocks = rows_dev // BLOCK
    first_blocks = (n_pblocks * 5 + 7) // 8
    bounds = [0, first_blocks * BLOCK, rows_dev] if 0 < first_blocks < n_pblocks else [0, rows_dev // 2, rows_dev]
    n_chunks = 2
    outs = None
    others = []
    for c in range(n_chunks):
        rows = slice(bounds[c], bounds[c + 1])
        theirs = project(their_rows[rows])
        mine = project(mine_rows[rows])
        sent = lax.ppermute(theirs, "section", partner)
        outs, grad = score(mine, sent, target_slot, block_lists, list_lens,
                           buf, tab_b, parity, tuple(aways), bounds[c], rows_dev, outs)
        others.append(lax.ppermute(grad, "section", partner))
    query_grad, loss_rows = outs
    position_loss = loss_rows.reshape(rows_dev)

    def to_trunk(g):
        return lax.dot_general(g, w_proj, (((1,), (1,)), ((), ())),
                               preferred_element_type=jnp.float32).astype(jnp.bfloat16)

    trunk_grad = jnp.zeros((halves, rows_dev, width_half), jnp.bfloat16)
    trunk_grad = lax.dynamic_update_slice(trunk_grad, to_trunk(query_grad)[None], (sec, 0, 0))
    for c in range(n_chunks):
        trunk_grad = lax.dynamic_update_slice(trunk_grad, to_trunk(others[c])[None], (1 - sec, bounds[c], 0))
    return (query_grad, position_loss, trunk_grad)


def solution(mesh):
    return jax.shard_map(
        shards,
        mesh=mesh,
        in_specs=(
            P(None, ("owner", "pos"), "section"),
            P("section", None),
            P(("section", "owner"), None),
            P(("section", "owner")),
            P(),
            P(("section", "owner", "pos")),
            P(("section", "owner", "pos"), None),
            P(("section", "owner", "pos")),
        ),
        out_specs=(
            P(("section", "owner", "pos"), None),
            P(("section", "owner", "pos")),
            P(None, ("owner", "pos"), "section"),
        ),
        check_vma=False,
    )
```

```python
import functools

import jax
import jax.numpy as jnp
from jax import lax
from jax.experimental import pallas as pl
from jax.experimental.pallas import tpu as pltpu
from jax.sharding import PartitionSpec as P


BLOCK = 256
NEG_FILL = -1e30
BIAS_ROWS = 16
GROUP = 4
EXT = BLOCK + 128


def score_kernel(list_width, n_blocks, aways, n_prev, first,
                 lists_ref, lens_ref, tgt_ref, par_ref,
                 qa_ref, qb_ref, tcol_ref, tab_a_ref, tab_b_ref, *refs):
    (qg_ref, loss_ref, qgc_ref, tabb_ref, tabf_ref, bias_ref, pos_ref, ls_ref, acc_ref, sem) = refs[n_prev:]
    _score_body(list_width, n_blocks, aways, first, lists_ref, lens_ref, tgt_ref, par_ref,
                qa_ref, qb_ref, tcol_ref, tab_a_ref, tab_b_ref, qg_ref, loss_ref, qgc_ref,
                tabb_ref, tabf_ref, bias_ref, pos_ref, ls_ref, acc_ref, sem)


def _score_body(list_width, n_blocks, aways, first,
                 lists_ref, lens_ref, tgt_ref, par_ref,
                 qa_ref, qb_ref, tcol_ref, tab_a_ref, tab_b_ref,
                 qg_ref, loss_ref, qgc_ref,
                 tabb_ref, tabf_ref, bias_ref, pos_ref, ls_ref, acc_ref, sem):
    b = pl.program_id(0)
    bg = b + first
    n_shards = tab_a_ref.shape[0]
    n_cand_blocks = 2 * n_shards

    def issue(block, slot):
        def one(r, carry):
            t = tgt_ref[(first + block) * BLOCK + r]
            pltpu.make_async_copy(tabf_ref.at[pl.ds(t, 1), :], pos_ref.at[slot, pl.ds(r, 1), :],
                                  sem.at[slot]).start()
            return carry

        lax.fori_loop(0, BLOCK, one, 0, unroll=8)

    @pl.when(b == 0)
    def _():
        mine = par_ref[0]
        me = par_ref[1]
        for s in range(n_shards):
            away = aways[s]
            for ref, par in ((tab_a_ref, mine), (tab_b_ref, 1 - mine)):
                j = 2 * (me ^ away) + par
                blk = ref[s, pl.ds(0, BLOCK), :]
                tabb_ref[j] = blk
                tabf_ref[pl.ds(pl.multiple_of(j * BLOCK, BLOCK), BLOCK), pl.ds(0, BLOCK)] = blk.astype(jnp.float32)
                extra = ref[s, pl.ds(BLOCK, BIAS_ROWS), :].astype(jnp.float32)
                bias_ref[pl.ds(j, 1), :] = extra[0:1]
        eye = (lax.broadcasted_iota(jnp.int32, (BLOCK, BLOCK), 0)
               == lax.broadcasted_iota(jnp.int32, (BLOCK, BLOCK), 1)).astype(jnp.float32)
        bias_col = lax.dot_general(eye, bias_ref[...], (((1,), (1,)), ((), ())),
                                   preferred_element_type=jnp.float32,
                                   precision=lax.Precision.HIGHEST)
        for j in range(n_cand_blocks):
            tabf_ref[pl.ds(j * BLOCK, BLOCK), pl.ds(BLOCK, 128)] = jnp.broadcast_to(
                bias_col[:, j:j + 1], (BLOCK, 128))
        issue(0, 0)

    slot = b % 2

    @pl.when(b + 1 < n_blocks)
    def _():
        issue(b + 1, 1 - slot)

    q = (qa_ref[...] + qb_ref[...]).astype(jnp.bfloat16)
    qf = q.astype(jnp.float32)
    tcol = tcol_ref[...]
    lane = lax.broadcasted_iota(jnp.int32, (BLOCK, BLOCK), 1)
    length = lens_ref[bg]
    n_groups = (length + GROUP - 1) // GROUP

    pltpu.make_async_copy(pos_ref.at[slot], pos_ref.at[slot], sem.at[slot]).wait()
    pos_ext = pos_ref[slot]
    positive = pos_ext[:, 0:BLOCK]
    pos_logit = jnp.sum(qf * positive, axis=1, keepdims=True) - pos_ext[:, BLOCK:BLOCK + 1]

    def pass_a(g, m):
        for i in range(GROUP):
            k = g * GROUP + i
            j = lists_ref[bg * list_width + k]
            cand = tabb_ref[j]
            logits = lax.dot_general(q, cand, (((1,), (1,)), ((), ())),
                                     preferred_element_type=jnp.float32) - bias_ref[pl.ds(j, 1), :]
            usable = jnp.logical_and((lane + j * BLOCK) != tcol, k < length)
            masked = jnp.where(usable, logits, NEG_FILL)
            ls_ref[k] = masked
            m = jnp.maximum(m, jnp.max(masked, axis=1, keepdims=True))
        return m

    m = lax.fori_loop(0, n_groups, pass_a, pos_logit)

    def pass_b(g, s):
        for i in range(GROUP):
            s = s + jnp.exp(ls_ref[g * GROUP + i] - m)
        return s

    s_vec = lax.fori_loop(0, n_groups, pass_b, jnp.zeros((BLOCK, BLOCK), jnp.float32))
    row_sum = jnp.exp(pos_logit - m) + jnp.sum(s_vec, axis=1, keepdims=True)
    log_total = m + jnp.log(row_sum)

    acc_ref[...] = jnp.zeros_like(acc_ref)

    def pass_c(g, carry):
        part = None
        for i in range(GROUP):
            k = g * GROUP + i
            j = lists_ref[bg * list_width + k]
            w = jnp.exp(ls_ref[k] - log_total).astype(jnp.bfloat16)
            d = jnp.dot(w, tabb_ref[j], preferred_element_type=jnp.float32)
            part = d if part is None else part + d
        acc_ref[...] += part
        return carry

    lax.fori_loop(0, n_groups, pass_c, 0)
    qg = acc_ref[...] + (jnp.exp(pos_logit - log_total) - 1.0) * positive
    qg_ref[...] = qg.astype(qg_ref.dtype)
    qgc_ref[...] = qg.astype(qgc_ref.dtype)
    loss_col = jnp.broadcast_to(log_total - pos_logit, (BLOCK, 128))
    loss_ref[...] = jnp.transpose(loss_col)[0:1, :].reshape(loss_ref.shape)


def score(q_mine, q_sent, target_slot, target_col, block_lists, list_lens, tab_a, tab_b, parity, aways,
          offset, total_rows, prev=None):
    rows, embed = q_mine.shape
    n_blocks = rows // BLOCK
    first = offset // BLOCK
    n_shards = tab_a.shape[0]
    n_cands = 2 * n_shards * BLOCK
    list_width = block_lists.shape[1]
    prev = () if prev is None else tuple(prev)
    grid_spec = pltpu.PrefetchScalarGridSpec(
        num_scalar_prefetch=4,
        grid=(n_blocks,),
        in_specs=[
            pl.BlockSpec((BLOCK, embed), lambda b, *_: (b, 0)),
            pl.BlockSpec((BLOCK, embed), lambda b, *_: (b, 0)),
            pl.BlockSpec((BLOCK, 1), lambda b, *_: (b + first, 0)),
            pl.BlockSpec(memory_space=pltpu.VMEM),
            pl.BlockSpec(memory_space=pltpu.VMEM),
        ] + [pl.BlockSpec(memory_space=pl.ANY)] * len(prev),
        out_specs=[
            pl.BlockSpec((BLOCK, embed), lambda b, *_: (b + first, 0)),
            pl.BlockSpec((1, 1, BLOCK), lambda b, *_: (b + first, 0, 0)),
            pl.BlockSpec((BLOCK, embed), lambda b, *_: (b, 0)),
        ],
        scratch_shapes=[
            pltpu.VMEM((2 * n_shards, BLOCK, embed), jnp.bfloat16),
            pltpu.VMEM((n_cands, EXT), jnp.float32),
            pltpu.VMEM((2 * n_shards, BLOCK), jnp.float32),
            pltpu.VMEM((2, BLOCK, EXT), jnp.float32),
            pltpu.VMEM((list_width, BLOCK, BLOCK), jnp.float32),
            pltpu.VMEM((BLOCK, embed), jnp.float32),
            pltpu.SemaphoreType.DMA((2,)),
        ],
    )
    flops = 2 * 2 * rows * embed * BLOCK * 8
    n_in = 4 + 5
    qg, loss, qg_chunk = pl.pallas_call(
        functools.partial(score_kernel, list_width, n_blocks, aways, len(prev), first),
        grid_spec=grid_spec,
        out_shape=[
            jax.ShapeDtypeStruct((total_rows, embed), jnp.bfloat16),
            jax.ShapeDtypeStruct((total_rows // BLOCK, 1, BLOCK), jnp.float32),
            jax.ShapeDtypeStruct((rows, embed), jnp.bfloat16),
        ],
        input_output_aliases={n_in + i: i for i in range(len(prev))},
        compiler_params=pltpu.CompilerParams(
            dimension_semantics=("arbitrary",),
            vmem_limit_bytes=62 * 1024 * 1024,
        ),
        cost_estimate=pl.CostEstimate(
            flops=flops, transcendentals=2 * rows * BLOCK * 8,
            bytes_accessed=2 * tab_a.size * 2 + rows * embed * 4),
    )(block_lists.reshape(-1), list_lens, target_slot, parity,
      q_mine, q_sent, target_col, tab_a, tab_b, *prev)
    return (qg, loss), qg_chunk


def shards(hidden_rows, w_proj, panels, cand_ids, counts, target_slot, block_lists, list_lens):
    halves, rows_dev, width_half = hidden_rows.shape
    n_sec = lax.axis_size("section")
    sec = lax.axis_index("section")
    partner = [(i, i ^ 1) for i in range(n_sec)]
    n_pos = lax.axis_size("pos")
    core = lax.axis_index("pos") % 2
    n_own = lax.axis_size("owner")
    me = sec * n_own + lax.axis_index("owner")
    own_bias = jnp.log(counts[cand_ids].astype(jnp.float32)).astype(jnp.bfloat16)
    own_bias = own_bias.reshape(panels.shape[0] // BLOCK, BLOCK)
    my_block = lax.dynamic_slice_in_dim(panels, core * BLOCK, BLOCK, axis=0)
    my_bias = jnp.pad(lax.dynamic_slice_in_dim(own_bias, core, 1, axis=0), ((0, BIAS_ROWS - 1), (0, 0)))
    buf = jnp.concatenate([my_block, my_bias], axis=0)[None]
    n_group = n_sec * n_own
    group = ("section", "owner")

    def swap(x, d):
        return lax.ppermute(x, group, [(i, i ^ d) for i in range(n_group)])

    if n_group == 16:
        got = [swap(buf, 4 * m) for m in range(1, 4)]
        buf = jnp.concatenate([buf] + got, axis=0)
        g1, g3 = swap(buf, 1), swap(buf, 3)
        h1, h2 = swap(g3[0:2], 1), swap(g1[2:4], 3)
        buf = jnp.concatenate([buf, g1, g3, h1, h2], axis=0)
        xs = [4 * k for k in range(4)]
        aways = xs + [1 ^ a for a in xs] + [3 ^ a for a in xs] + [2 ^ a for a in xs]
    else:
        aways = [0]
        d = n_group // 2
        while d >= 1:
            buf = jnp.concatenate([buf, swap(buf, d)], axis=0)
            aways = aways + [d ^ a for a in aways]
            d //= 2
    tab_b = lax.ppermute(buf, "pos", [(i, i ^ 1) for i in range(n_pos)])
    parity = jnp.stack([core, me]).astype(jnp.int32)
    mine_rows = lax.dynamic_index_in_dim(hidden_rows, sec, 0, keepdims=False)
    their_rows = lax.dynamic_index_in_dim(hidden_rows, 1 - sec, 0, keepdims=False)

    def project(x):
        return jnp.dot(x, w_proj, preferred_element_type=jnp.float32)

    n_pblocks = rows_dev // BLOCK
    first_blocks = (n_pblocks * 5 + 7) // 8
    bounds = [0, first_blocks * BLOCK, rows_dev] if 0 < first_blocks < n_pblocks else [0, rows_dev // 2, rows_dev]
    n_chunks = 2
    target_col = target_slot.reshape(rows_dev, 1)
    outs = None
    others = []
    for c in range(n_chunks):
        rows = slice(bounds[c], bounds[c + 1])
        theirs = project(their_rows[rows])
        mine = project(mine_rows[rows])
        sent = lax.ppermute(theirs, "section", partner)
        outs, grad = score(mine, sent, target_slot, target_col, block_lists, list_lens,
                           buf, tab_b, parity, tuple(aways), bounds[c], rows_dev, outs)
        others.append(lax.ppermute(grad, "section", partner))
    query_grad, loss_rows = outs
    position_loss = loss_rows.reshape(rows_dev)

    def to_trunk(g):
        return lax.dot_general(g, w_proj, (((1,), (1,)), ((), ())),
                               preferred_element_type=jnp.float32).astype(jnp.bfloat16)

    trunk_grad = jnp.zeros((halves, rows_dev, width_half), jnp.bfloat16)
    trunk_grad = lax.dynamic_update_slice(trunk_grad, to_trunk(query_grad)[None], (sec, 0, 0))
    for c in range(n_chunks):
        trunk_grad = lax.dynamic_update_slice(trunk_grad, to_trunk(others[c])[None], (1 - sec, bounds[c], 0))
    return (query_grad, position_loss, trunk_grad)


def solution(mesh):
    return jax.shard_map(
        shards,
        mesh=mesh,
        in_specs=(
            P(None, ("owner", "pos"), "section"),
            P("section", None),
            P(("section", "owner"), None),
            P(("section", "owner")),
            P(),
            P(("section", "owner", "pos")),
            P(("section", "owner", "pos"), None),
            P(("section", "owner", "pos")),
        ),
        out_specs=(
            P(("section", "owner", "pos"), None),
            P(("section", "owner", "pos")),
            P(None, ("owner", "pos"), "section"),
        ),
        check_vma=False,
    )
```
